128 devices in a mesh: px: 8 (over x_lo, z), py: 16 (over x_hi, y, core).
Axes of the slice: x: 4 (x_hi: 2, x_lo: 2; x = x_hi * 2 + x_lo), y: 4, z: 4, core: 2. Of those that a mesh axis runs over, the one named last changes fastest.
Arguments:
- widths: float32 [2048, 4096], P('px', 'py'), may hold values from -1 to 1
- couplings: int32 [256, 512, 9], P('px', 'py'), may hold values 0 or 1
- surrogate: bfloat16 [9, 256, 1024], replicated, may hold values from -0.375 to 0.375
- target_far: bfloat16 [2048, 8, 2, 512], P(('px', 'py')), may hold values from -6 to 6
Outputs:
- far_field: float32 [2048, 8, 2, 512], P(('px', 'py'))
- width_grad: float32 [2048, 4096], P('px', 'py')
The draws below stay inside these ranges and needn't reach their ends.
All inputs are finite; a program needn't handle non-finite values. No bound on the sum of `couplings` on one device may be relied on, other than what follows from the above.
Results may differ from the reference program's by a relative error of at most 0.0033.
The reference program's roundings to bfloat16 on the way count: a program that leaves them out, or rounds other values in their place, can miss the bound.
Values may be sent and summed in bfloat16 or wider, within the bound.
No kernel may reach another device: no remote copies, remote signals or barrier semaphores. Data moves between devices by JAX's collectives and lax.ppermute only.
A program may use at most 128 MiB of HBM per device.

```python
import math
import jax
import jax.numpy as jnp
from jax import lax

BS = 8
NF = 4
NW = 8
NK = 512
NX = 2048
NY = 4096
NBX = 256
NBY = 512
FEAT = 256
OUTS = 1024


def plant(entries, stream_key, least, top_value):
    longest = entries.shape.index(max(entries.shape))
    spots = []
    for shift in (0, 1):
        where = [jax.random.randint(jax.random.fold_in(stream_key, axis), (), 0, length) for axis, length in enumerate(entries.shape)]
        where[longest] = (where[longest] + shift) % entries.shape[longest]
        spots.append(tuple(where))
    return entries.at[spots[0]].set(least).at[spots[1]].set(top_value)


def shard_levels(stream_key, dims, pieces, least, top_value):
    level = 1.0
    for dim, blocks in pieces:
        steps = jax.random.uniform(jax.random.fold_in(jax.random.fold_in(stream_key, 6), dim), (blocks,), jnp.float32, least / len(pieces), top_value / len(pieces))
        level = level * jnp.repeat(jnp.exp(steps), dims[dim] // blocks).reshape((-1,) + (1,) * (len(dims) - 1 - dim))
    return level


def noise(rng, extent, width, limit, shards=(), held_as=jnp.bfloat16):
    level = shard_levels(rng, extent, shards, -0.22, 0.18) if shards else 1.0
    drawn = jax.random.normal(rng, extent, jnp.float32) * width * level
    return jnp.minimum(jnp.maximum(drawn, -limit), limit).astype(held_as)


def setup_inputs(seed: int = 0) -> dict:
    streams_of = jax.random.split(jax.random.key(seed), 5)
    widths = jnp.clip(jax.random.uniform(streams_of[0], (NX, NY), jnp.float32, -1.0, 1.0) * shard_levels(streams_of[0], (NX, NY), ((0, 8), (1, 16)), -0.4, 0.0), -1.0, 1.0)
    couplings = plant((jax.random.randint(streams_of[1], (NBX, NBY, 9), 0, 4) < 3).astype(jnp.int32), jax.random.fold_in(streams_of[1], 1), 0, 1)
    surrogate = noise(streams_of[2], (9, FEAT, OUTS), FEAT ** -0.5, 0.375)
    target_far = noise(streams_of[3], (NX, NW, 2, NK), 1.0, 6.0, ((0, 128),))
    return {"widths": widths, "couplings": couplings, "surrogate": surrogate, "target_far": target_far}


tv_weight = 0.5
tv_floor = 0.01

def chebyshev(normed, levels):
    values, slopes = ([], [])
    before = jnp.ones_like(normed)
    current = normed
    slope_before = jnp.zeros_like(normed)
    slope_now = jnp.ones_like(normed)
    for level in range(levels):
        values.append(current)
        slopes.append(slope_now)
        follow = 2.0 * normed * current - before
        slope_follow = 2.0 * current + 2.0 * normed * slope_now - slope_before
        before, current, slope_before, slope_now = (current, follow, slope_now, slope_follow)
    return (jnp.stack(values, 1), jnp.stack(slopes, 1))

def cell_blocks(planes, block_side):
    height, layers, columns = planes.shape
    shaped = planes.reshape(height // block_side, block_side, layers, columns // block_side, block_side)
    return shaped.transpose(0, 3, 1, 2, 4).reshape(height // block_side, columns // block_side, block_side * layers * block_side)

def block_cells(blocks, block_side, layers):
    block_rows, block_cols, unused = blocks.shape
    shaped = blocks.reshape(block_rows, block_cols, block_side, layers, block_side)
    return shaped.transpose(0, 2, 3, 1, 4).reshape(block_rows * block_side, layers, block_cols * block_side)

def field_rows(blocks, block_side, wave_count):
    block_rows, block_cols, unused = blocks.shape
    shaped = blocks.reshape(block_rows, block_cols, block_side, wave_count, 2 * block_side)
    return shaped.transpose(0, 2, 3, 1, 4).reshape(block_rows * block_side * wave_count, block_cols * 2 * block_side)

def rows_field(row_flat, block_side, wave_count):
    row_count, unused = row_flat.shape
    height = row_count // wave_count
    block_cols = unused // (2 * block_side)
    shaped = row_flat.reshape(height // block_side, block_side, wave_count, block_cols, 2 * block_side)
    return shaped.transpose(0, 3, 1, 2, 4).reshape(height // block_side, block_cols, block_side * wave_count * 2 * block_side)

def phase_table(first_col, col_count, total_cols):
    places = first_col + jnp.arange(col_count, dtype=jnp.int32)
    orders = jnp.arange(NK, dtype=jnp.int32) - NK // 2
    phase_turns = places[:, None] * orders[None, :] % total_cols
    angles = phase_turns.astype(jnp.float32) * (2.0 * math.pi / total_cols)
    cosine = jnp.cos(angles)
    sine_part = jnp.sin(angles)
    phase_rows = jnp.stack([jnp.stack([cosine, -sine_part], 1), jnp.stack([sine_part, cosine], 1)], 1)
    phase_rows = phase_rows.astype(jnp.bfloat16).reshape(col_count // BS, BS, 2, 2 * NK)
    return phase_rows.transpose(0, 2, 1, 3).reshape(2 * col_count, 2 * NK)

def variation(framed, row_first, col_first, total_rows, total_cols):
    height = framed.shape[0] - 2
    columns = framed.shape[1] - 2
    step_down = framed[1:, :-1] - framed[:-1, :-1]
    step_right = framed[:-1, 1:] - framed[:-1, :-1]
    row_at = row_first - 1 + jnp.arange(height + 1, dtype=jnp.int32)
    col_at = col_first - 1 + jnp.arange(columns + 1, dtype=jnp.int32)
    step_down = jnp.where(((row_at >= 0) & (row_at < total_rows - 1))[:, None], step_down, 0.0)
    step_right = jnp.where(((col_at >= 0) & (col_at < total_cols - 1))[None, :], step_right, 0.0)
    magnitude = jnp.sqrt(step_down * step_down + step_right * step_right + tv_floor)
    flow_down = step_down / magnitude
    flow_right = step_right / magnitude
    return -(flow_down + flow_right)[1:, 1:] + flow_down[:-1, 1:] + flow_right[1:, :-1]

def reference(widths, couplings, surrogate, target_far):
    values, slopes = chebyshev(widths, NF)
    features = cell_blocks(values, BS).astype(jnp.bfloat16)
    feat_pad = jnp.pad(features, ((1, 1), (1, 1), (0, 0)))
    mask_pad = jnp.pad(couplings, ((1, 1), (1, 1), (0, 0))).astype(jnp.float32)
    gathered = jnp.zeros((NBX, NBY, OUTS), jnp.float32)
    for row_step in range(3):
        for col_step in range(3):
            offset = row_step * 3 + col_step
            source = feat_pad[2 - row_step:2 - row_step + NBX, 2 - col_step:2 - col_step + NBY]
            product = jnp.dot(source.reshape(NBX * NBY, FEAT), surrogate[offset], preferred_element_type=jnp.float32)
            flags = mask_pad[2 - row_step:2 - row_step + NBX, 2 - col_step:2 - col_step + NBY, offset]
            gathered = gathered + flags[:, :, None] * product.reshape(NBX, NBY, OUTS)
    near_field = gathered.astype(jnp.bfloat16)
    row_flat = field_rows(near_field, BS, NW)
    phase_rows = phase_table(0, NY, NY)
    norm_scale = 1.0 / math.sqrt(NY)
    far_field = (jnp.dot(row_flat, phase_rows, preferred_element_type=jnp.float32) * norm_scale).reshape(NX, NW, 2, NK)
    far_miss = (far_field - target_far.astype(jnp.float32)).astype(jnp.bfloat16)
    adj_flat = jnp.dot(far_miss.reshape(NX * NW, 2 * NK), phase_rows.T, preferred_element_type=jnp.float32) * norm_scale
    adj_blocks = rows_field(adj_flat.astype(jnp.bfloat16), BS, NW)
    adj_pad = jnp.pad(adj_blocks, ((1, 1), (1, 1), (0, 0)))
    feat_grad = jnp.zeros((NBX, NBY, FEAT), jnp.float32)
    for row_step in range(3):
        for col_step in range(3):
            offset = row_step * 3 + col_step
            targets_at = adj_pad[row_step:row_step + NBX, col_step:col_step + NBY]
            product = jnp.dot(targets_at.reshape(NBX * NBY, OUTS), surrogate[offset].T, preferred_element_type=jnp.float32)
            flags = couplings[:, :, offset].astype(jnp.float32)
            feat_grad = feat_grad + flags[:, :, None] * product.reshape(NBX, NBY, FEAT)
    planes = block_cells(feat_grad, BS, NF)
    near_grad = lax.optimization_barrier(jnp.sum(planes * slopes, axis=1))
    framed = jnp.pad(widths, ((1, 1), (1, 1)))
    grad_tv = variation(framed, 0, 0, NX, NY)
    return (far_field, near_grad + tv_weight * grad_tv)
```

```python
import math

import jax
import jax.numpy as jnp
from jax import lax
from jax.sharding import PartitionSpec as P

BS = 8
NF = 4
NW = 8
NK = 512
FEAT = 256
OUTS = 1024


tv_weight = 0.5
tv_floor = 0.01


def with_halo(block, sides, width):
    for axis, dim in sides:
        count = lax.axis_size(axis)
        forward = [(i, i + 1) for i in range(count - 1)]
        backward = [(target, source) for source, target in forward]
        low = lax.ppermute(
            lax.slice_in_dim(block, block.shape[dim] - width, None, axis=dim), axis, forward
        )
        high = lax.ppermute(lax.slice_in_dim(block, 0, width, axis=dim), axis, backward)
        block = jnp.concatenate([low, block, high], axis=dim)
    return block


def chebyshev(normed, levels):
    values, slopes = ([], [])
    before = jnp.ones_like(normed)
    current = normed
    slope_before = jnp.zeros_like(normed)
    slope_now = jnp.ones_like(normed)
    for level in range(levels):
        values.append(current)
        slopes.append(slope_now)
        follow = 2.0 * normed * current - before
        slope_follow = 2.0 * current + 2.0 * normed * slope_now - slope_before
        before, current, slope_before, slope_now = (current, follow, slope_now, slope_follow)
    return (jnp.stack(values, 1), jnp.stack(slopes, 1))


def cell_blocks(planes, block_side):
    height, layers, columns = planes.shape
    shaped = planes.reshape(
        height // block_side, block_side, layers, columns // block_side, block_side
    )
    return shaped.transpose(0, 3, 1, 2, 4).reshape(
        height // block_side, columns // block_side, block_side * layers * block_side
    )


def block_cells(blocks, block_side, layers):
    block_rows, block_cols, unused = blocks.shape
    shaped = blocks.reshape(block_rows, block_cols, block_side, layers, block_side)
    return shaped.transpose(0, 2, 3, 1, 4).reshape(
        block_rows * block_side, layers, block_cols * block_side
    )


def field_rows(blocks, block_side, wave_count):
    block_rows, block_cols, unused = blocks.shape
    shaped = blocks.reshape(block_rows, block_cols, block_side, wave_count, 2 * block_side)
    return shaped.transpose(0, 2, 3, 1, 4).reshape(
        block_rows * block_side * wave_count, block_cols * 2 * block_side
    )


def rows_field(row_flat, block_side, wave_count):
    row_count, unused = row_flat.shape
    height = row_count // wave_count
    block_cols = unused // (2 * block_side)
    shaped = row_flat.reshape(
        height // block_side, block_side, wave_count, block_cols, 2 * block_side
    )
    return shaped.transpose(0, 3, 1, 2, 4).reshape(
        height // block_side, block_cols, block_side * wave_count * 2 * block_side
    )


def phase_table(first_col, col_count, total_cols):
    places = first_col + jnp.arange(col_count, dtype=jnp.int32)
    orders = jnp.arange(NK, dtype=jnp.int32) - NK // 2
    phase_turns = places[:, None] * orders[None, :] % total_cols
    angles = phase_turns.astype(jnp.float32) * (2.0 * math.pi / total_cols)
    cosine = jnp.cos(angles)
    sine_part = jnp.sin(angles)
    phase_rows = jnp.stack(
        [jnp.stack([cosine, -sine_part], 1), jnp.stack([sine_part, cosine], 1)], 1
    )
    phase_rows = phase_rows.astype(jnp.bfloat16).reshape(col_count // BS, BS, 2, 2 * NK)
    return phase_rows.transpose(0, 2, 1, 3).reshape(2 * col_count, 2 * NK)


def variation(framed, row_first, col_first, total_rows, total_cols):
    height = framed.shape[0] - 2
    columns = framed.shape[1] - 2
    step_down = framed[1:, :-1] - framed[:-1, :-1]
    step_right = framed[:-1, 1:] - framed[:-1, :-1]
    row_at = row_first - 1 + jnp.arange(height + 1, dtype=jnp.int32)
    col_at = col_first - 1 + jnp.arange(columns + 1, dtype=jnp.int32)
    step_down = jnp.where(((row_at >= 0) & (row_at < total_rows - 1))[:, None], step_down, 0.0)
    step_right = jnp.where(((col_at >= 0) & (col_at < total_cols - 1))[None, :], step_right, 0.0)
    magnitude = jnp.sqrt(step_down * step_down + step_right * step_right + tv_floor)
    flow_down = step_down / magnitude
    flow_right = step_right / magnitude
    return -(flow_down + flow_right)[1:, 1:] + flow_down[:-1, 1:] + flow_right[1:, :-1]


def lane_perm():
    rows = lax.broadcasted_iota(jnp.int32, (OUTS, OUTS), 0)
    cols = lax.broadcasted_iota(jnp.int32, (OUTS, OUTS), 1)
    inner = NW * BS
    hit = (rows // (2 * BS) == cols % inner) & (rows % (2 * BS) == cols // inner)
    return hit.astype(jnp.bfloat16)


def dft_table(total_cols):
    kk = jnp.arange(NK, dtype=jnp.int32) - NK // 2
    low = 8 * BS
    high = total_cols // low
    a = jnp.arange(high, dtype=jnp.int32)
    b = jnp.arange(low, dtype=jnp.int32)
    scale = 2.0 * math.pi / total_cols
    ta = ((a[:, None] * low * kk[None, :]) % total_cols).astype(jnp.float32) * scale
    tb = ((b[:, None] * kk[None, :]) % total_cols).astype(jnp.float32) * scale
    ca, sa = jnp.cos(ta), jnp.sin(ta)
    cb, sb = jnp.cos(tb), jnp.sin(tb)
    cb = cb.reshape(BS, BS, NK).transpose(1, 0, 2)
    sb = sb.reshape(BS, BS, NK).transpose(1, 0, 2)
    cos_v = ca[None, :, None, :] * cb[:, None, :, :] - sa[None, :, None, :] * sb[:, None, :, :]
    sin_v = sa[None, :, None, :] * cb[:, None, :, :] + ca[None, :, None, :] * sb[:, None, :, :]
    cos_v = cos_v.reshape(BS, total_cols // BS, NK)
    sin_v = sin_v.reshape(BS, total_cols // BS, NK)
    first = jnp.concatenate([cos_v, -sin_v], axis=-1)
    second = jnp.concatenate([sin_v, cos_v], axis=-1)
    table = jnp.stack([first, second]).astype(jnp.bfloat16)
    return table.reshape(2 * BS, total_cols // BS, 2 * NK)


def per_device(widths, couplings, surrogate, target_far):
    height, columns = widths.shape
    block_rows = height // BS
    block_cols = columns // BS
    groups = lax.axis_size("py")
    total_cols = columns * groups
    total_rows = height * lax.axis_size("px")
    mask_cells = jnp.pad(couplings.astype(jnp.float32), ((0, 0), (0, 0), (0, BS * BS - 9)))
    mask_cells = (
        mask_cells.reshape(block_rows, block_cols, BS, BS)
        .transpose(0, 2, 1, 3)
        .reshape(height, columns)
    )
    rimmed = with_halo(jnp.stack([widths, mask_cells]), (("px", 1), ("py", 2)), BS)
    wide_widths = rimmed[0]
    wide_mask = rimmed[1].reshape(block_rows + 2, BS, block_cols + 2, BS).transpose(0, 2, 1, 3)
    wide_mask = wide_mask.reshape(block_rows + 2, block_cols + 2, BS * BS).astype(jnp.bfloat16)
    values, slopes = chebyshev(wide_widths, NF)
    own_slopes = slopes[BS : BS + height, :, BS : BS + columns]
    features = cell_blocks(values, BS).astype(jnp.bfloat16)
    pieces = []
    for row_step in range(3):
        for col_step in range(3):
            offset = row_step * 3 + col_step
            source = features[
                2 - row_step : 2 - row_step + block_rows, 2 - col_step : 2 - col_step + block_cols
            ]
            flags = wide_mask[
                2 - row_step : 2 - row_step + block_rows,
                2 - col_step : 2 - col_step + block_cols,
                offset,
            ]
            pieces.append(source * flags[:, :, None])
    stacked = jnp.concatenate(pieces, axis=-1).reshape(block_rows * block_cols, 9 * FEAT)
    near_field = jnp.dot(
        stacked, surrogate.reshape(9 * FEAT, OUTS), preferred_element_type=jnp.float32
    ).astype(jnp.bfloat16)
    perm = lane_perm()
    near_perm = jnp.dot(near_field, perm, preferred_element_type=jnp.float32).astype(jnp.bfloat16)
    near_perm = near_perm.reshape(block_rows, block_cols, OUTS)
    own_rows = lax.all_to_all(near_perm, "py", 0, 1, tiled=True)
    own_bx = own_rows.shape[0]
    all_by = own_rows.shape[1]
    table = dft_table(total_cols)
    norm_scale = 1.0 / math.sqrt(total_cols)
    lhs = own_rows.reshape(own_bx, all_by, 2 * BS, NW * BS)
    far_flat = jnp.einsum("bYpi,pYq->biq", lhs, table, preferred_element_type=jnp.float32)
    far_field = (far_flat * norm_scale).reshape(own_bx * BS, NW, 2, NK)
    far_miss = (far_field - target_far.astype(jnp.float32)).astype(jnp.bfloat16)
    miss_flat = far_miss.reshape(own_bx, NW * BS, 2 * NK)
    adj_flat = jnp.einsum("biq,pYq->bYpi", miss_flat, table, preferred_element_type=jnp.float32)
    adj_perm = (adj_flat * norm_scale).astype(jnp.bfloat16).reshape(own_bx, all_by, OUTS)
    adj_back = lax.all_to_all(adj_perm, "py", 1, 0, tiled=True)
    adj_blocks = jnp.einsum(
        "bc,rc->br", adj_back.reshape(block_rows * block_cols, OUTS), perm,
        preferred_element_type=jnp.float32,
    ).astype(jnp.bfloat16).reshape(block_rows, block_cols, OUTS)
    wide_adj = with_halo(adj_blocks, (("px", 0), ("py", 1)), 1)
    feat_grad = jnp.zeros((block_rows, block_cols, FEAT), jnp.float32)
    for row_step in range(3):
        for col_step in range(3):
            offset = row_step * 3 + col_step
            targets_at = wide_adj[
                row_step : row_step + block_rows, col_step : col_step + block_cols
            ]
            product = jnp.dot(
                targets_at.reshape(block_rows * block_cols, OUTS),
                surrogate[offset].T,
                preferred_element_type=jnp.float32,
            )
            flags = couplings[:, :, offset].astype(jnp.float32)
            feat_grad = feat_grad + flags[:, :, None] * product.reshape(
                block_rows, block_cols, FEAT
            )
    planes = block_cells(feat_grad, BS, NF)
    near_grad = jnp.sum(planes * own_slopes, axis=1)
    framed = wide_widths[BS - 1 : BS + height + 1, BS - 1 : BS + columns + 1]
    grad_tv = variation(
        framed,
        lax.axis_index("px") * height,
        lax.axis_index("py") * columns,
        total_rows,
        total_cols,
    )
    return (far_field, near_grad + tv_weight * grad_tv)


def solution(mesh):
    return jax.shard_map(
        per_device,
        mesh=mesh,
        in_specs=(P("px", "py"), P("px", "py", None), P(), P(("px", "py"), None, None, None)),
        out_specs=(P(("px", "py"), None, None, None), P("px", "py")),
        check_vma=False,
    )
```

```python
import math

import jax
import jax.numpy as jnp
from jax import lax
from jax.sharding import PartitionSpec as P

BS = 8
NF = 4
NW = 8
NK = 512
FEAT = 256
OUTS = 1024


tv_weight = 0.5
tv_floor = 0.01


def with_halo(block, sides, width):
    for axis, dim in sides:
        count = lax.axis_size(axis)
        forward = [(i, i + 1) for i in range(count - 1)]
        backward = [(target, source) for source, target in forward]
        low = lax.ppermute(
            lax.slice_in_dim(block, block.shape[dim] - width, None, axis=dim), axis, forward
        )
        high = lax.ppermute(lax.slice_in_dim(block, 0, width, axis=dim), axis, backward)
        block = jnp.concatenate([low, block, high], axis=dim)
    return block


def chebyshev(normed, levels):
    values, slopes = ([], [])
    before = jnp.ones_like(normed)
    current = normed
    slope_before = jnp.zeros_like(normed)
    slope_now = jnp.ones_like(normed)
    for level in range(levels):
        values.append(current)
        slopes.append(slope_now)
        follow = 2.0 * normed * current - before
        slope_follow = 2.0 * current + 2.0 * normed * slope_now - slope_before
        before, current, slope_before, slope_now = (current, follow, slope_now, slope_follow)
    return (jnp.stack(values, 1), jnp.stack(slopes, 1))


def cell_blocks(planes, block_side):
    height, layers, columns = planes.shape
    shaped = planes.reshape(
        height // block_side, block_side, layers, columns // block_side, block_side
    )
    return shaped.transpose(0, 3, 1, 2, 4).reshape(
        height // block_side, columns // block_side, block_side * layers * block_side
    )


def block_cells(blocks, block_side, layers):
    block_rows, block_cols, unused = blocks.shape
    shaped = blocks.reshape(block_rows, block_cols, block_side, layers, block_side)
    return shaped.transpose(0, 2, 3, 1, 4).reshape(
        block_rows * block_side, layers, block_cols * block_side
    )


def field_rows(blocks, block_side, wave_count):
    block_rows, block_cols, unused = blocks.shape
    shaped = blocks.reshape(block_rows, block_cols, block_side, wave_count, 2 * block_side)
    return shaped.transpose(0, 2, 3, 1, 4).reshape(
        block_rows * block_side * wave_count, block_cols * 2 * block_side
    )


def rows_field(row_flat, block_side, wave_count):
    row_count, unused = row_flat.shape
    height = row_count // wave_count
    block_cols = unused // (2 * block_side)
    shaped = row_flat.reshape(
        height // block_side, block_side, wave_count, block_cols, 2 * block_side
    )
    return shaped.transpose(0, 3, 1, 2, 4).reshape(
        height // block_side, block_cols, block_side * wave_count * 2 * block_side
    )


def phase_table(first_col, col_count, total_cols):
    places = first_col + jnp.arange(col_count, dtype=jnp.int32)
    orders = jnp.arange(NK, dtype=jnp.int32) - NK // 2
    phase_turns = places[:, None] * orders[None, :] % total_cols
    angles = phase_turns.astype(jnp.float32) * (2.0 * math.pi / total_cols)
    cosine = jnp.cos(angles)
    sine_part = jnp.sin(angles)
    phase_rows = jnp.stack(
        [jnp.stack([cosine, -sine_part], 1), jnp.stack([sine_part, cosine], 1)], 1
    )
    phase_rows = phase_rows.astype(jnp.bfloat16).reshape(col_count // BS, BS, 2, 2 * NK)
    return phase_rows.transpose(0, 2, 1, 3).reshape(2 * col_count, 2 * NK)


def variation(framed, row_first, col_first, total_rows, total_cols):
    height = framed.shape[0] - 2
    columns = framed.shape[1] - 2
    step_down = framed[1:, :-1] - framed[:-1, :-1]
    step_right = framed[:-1, 1:] - framed[:-1, :-1]
    row_at = row_first - 1 + jnp.arange(height + 1, dtype=jnp.int32)
    col_at = col_first - 1 + jnp.arange(columns + 1, dtype=jnp.int32)
    step_down = jnp.where(((row_at >= 0) & (row_at < total_rows - 1))[:, None], step_down, 0.0)
    step_right = jnp.where(((col_at >= 0) & (col_at < total_cols - 1))[None, :], step_right, 0.0)
    magnitude = jnp.sqrt(step_down * step_down + step_right * step_right + tv_floor)
    flow_down = step_down / magnitude
    flow_right = step_right / magnitude
    return -(flow_down + flow_right)[1:, 1:] + flow_down[:-1, 1:] + flow_right[1:, :-1]


def lane_perm():
    rows = lax.broadcasted_iota(jnp.int32, (OUTS, OUTS), 0)
    cols = lax.broadcasted_iota(jnp.int32, (OUTS, OUTS), 1)
    inner = NW * BS
    hit = (rows // (2 * BS) == cols % inner) & (rows % (2 * BS) == cols // inner)
    return hit.astype(jnp.bfloat16)


def dft_table(total_cols):
    kk = jnp.arange(NK, dtype=jnp.int32) - NK // 2
    low = 8 * BS
    high = total_cols // low
    a = jnp.arange(high, dtype=jnp.int32)
    b = jnp.arange(low, dtype=jnp.int32)
    scale = 2.0 * math.pi / total_cols
    ta = ((a[:, None] * low * kk[None, :]) % total_cols).astype(jnp.float32) * scale
    tb = ((b[:, None] * kk[None, :]) % total_cols).astype(jnp.float32) * scale
    ca, sa = jnp.cos(ta), jnp.sin(ta)
    cb, sb = jnp.cos(tb), jnp.sin(tb)
    cb = cb.reshape(BS, BS, NK).transpose(1, 0, 2)
    sb = sb.reshape(BS, BS, NK).transpose(1, 0, 2)
    cos_v = ca[None, :, None, :] * cb[:, None, :, :] - sa[None, :, None, :] * sb[:, None, :, :]
    sin_v = sa[None, :, None, :] * cb[:, None, :, :] + ca[None, :, None, :] * sb[:, None, :, :]
    cos_v = cos_v.reshape(BS, total_cols // BS, NK)
    sin_v = sin_v.reshape(BS, total_cols // BS, NK)
    return jnp.concatenate([cos_v, sin_v], axis=-1).astype(jnp.bfloat16)


def to_blocks(cells):
    rows, cols = cells.shape
    shaped = cells.reshape(rows // BS, BS, cols // BS, BS).transpose(0, 2, 1, 3)
    return shaped.reshape(rows // BS, cols // BS, BS * BS)


def to_cells(blocks):
    rows, cols, unused = blocks.shape
    shaped = blocks.reshape(rows, cols, BS, BS).transpose(0, 2, 1, 3)
    return shaped.reshape(rows * BS, cols * BS)


def chebyshev_terms(normed, levels):
    values, slopes = ([], [])
    before = jnp.ones_like(normed)
    current = normed
    slope_before = jnp.zeros_like(normed)
    slope_now = jnp.ones_like(normed)
    for level in range(levels):
        values.append(current)
        slopes.append(slope_now)
        follow = 2.0 * normed * current - before
        slope_follow = 2.0 * current + 2.0 * normed * slope_now - slope_before
        before, current, slope_before, slope_now = (current, follow, slope_now, slope_follow)
    return values, slopes


def per_device(widths, couplings, surrogate, target_far):
    height, columns = widths.shape
    block_rows = height // BS
    block_cols = columns // BS
    groups = lax.axis_size("py")
    total_cols = columns * groups
    total_rows = height * lax.axis_size("px")
    wide_widths = with_halo(widths, (("px", 0), ("py", 1)), BS)
    wide_flags = with_halo(couplings.astype(jnp.bfloat16), (("px", 0), ("py", 1)), 1)
    values, slopes = chebyshev_terms(to_blocks(wide_widths), NF)
    features = jnp.concatenate(values, axis=-1).astype(jnp.bfloat16)
    own_slopes = jnp.stack([s[1 : block_rows + 1, 1 : block_cols + 1] for s in slopes], axis=2)
    sur = surrogate.reshape(9, BS, NF, BS, OUTS).transpose(0, 2, 1, 3, 4).reshape(9, FEAT, OUTS)
    wide_cols = block_cols + 2
    cells = (block_rows + 2) * wide_cols
    flat = jnp.pad(features.reshape(cells, FEAT), ((1, 1), (0, 0)))
    flat_flags = jnp.pad(wide_flags.reshape(cells, 9), ((1, 1), (0, 0)))
    span = block_rows * wide_cols
    pieces = []
    for row_step in range(3):
        for col_step in range(3):
            offset = row_step * 3 + col_step
            first = (2 - row_step) * wide_cols + (2 - col_step)
            pieces.append(
                flat[first : first + span] * flat_flags[first : first + span, offset : offset + 1]
            )
    stacked = jnp.concatenate(pieces, axis=-1)
    near_field = jnp.dot(
        stacked, sur.reshape(9 * FEAT, OUTS), preferred_element_type=jnp.float32
    ).astype(jnp.bfloat16)
    near_field = near_field.reshape(block_rows, wide_cols, OUTS)[:, 1 : block_cols + 1]
    perm = lane_perm()
    near_perm = jnp.dot(
        near_field.reshape(block_rows * block_cols, OUTS), perm, preferred_element_type=jnp.float32
    ).astype(jnp.bfloat16)
    near_perm = near_perm.reshape(block_rows, block_cols, OUTS)
    own_rows = lax.all_to_all(near_perm, "py", 0, 1, tiled=True)
    own_bx = own_rows.shape[0]
    all_by = own_rows.shape[1]
    table = dft_table(total_cols)
    norm_scale = 1.0 / math.sqrt(total_cols)
    lhs = own_rows.reshape(own_bx, all_by, 2, BS, NW * BS)
    parts = jnp.einsum("bYpji,jYq->bpiq", lhs, table, preferred_element_type=jnp.float32)
    real = parts[:, 0, :, :NK] + parts[:, 1, :, NK:]
    imag = parts[:, 1, :, :NK] - parts[:, 0, :, NK:]
    far_field = (jnp.stack([real, imag], axis=2) * norm_scale).reshape(own_bx * BS, NW, 2, NK)
    far_miss = (far_field - target_far.astype(jnp.float32)).astype(jnp.bfloat16)
    miss = far_miss.reshape(own_bx, NW * BS, 2, NK)
    miss_re = miss[:, :, 0]
    miss_im = miss[:, :, 1]
    rhs = jnp.stack(
        [
            jnp.concatenate([miss_re, -miss_im], axis=-1),
            jnp.concatenate([miss_im, miss_re], axis=-1),
        ],
        axis=1,
    )
    adj_flat = jnp.einsum("bpiq,jYq->bYpji", rhs, table, preferred_element_type=jnp.float32)
    adj_perm = (adj_flat * norm_scale).astype(jnp.bfloat16).reshape(own_bx, all_by, OUTS)
    adj_back = lax.all_to_all(adj_perm, "py", 1, 0, tiled=True)
    adj_blocks = jnp.einsum(
        "bc,rc->br", adj_back.reshape(block_rows * block_cols, OUTS), perm,
        preferred_element_type=jnp.float32,
    ).astype(jnp.bfloat16).reshape(block_rows, block_cols, OUTS)
    wide_adj = with_halo(adj_blocks, (("px", 0), ("py", 1)), 1)
    feat_grad = jnp.zeros((block_rows, block_cols, FEAT), jnp.float32)
    for row_step in range(3):
        for col_step in range(3):
            offset = row_step * 3 + col_step
            targets_at = wide_adj[
                row_step : row_step + block_rows, col_step : col_step + block_cols
            ]
            product = jnp.dot(
                targets_at.reshape(block_rows * block_cols, OUTS),
                sur[offset].T,
                preferred_element_type=jnp.float32,
            )
            flags = couplings[:, :, offset].astype(jnp.float32)
            feat_grad = feat_grad + flags[:, :, None] * product.reshape(
                block_rows, block_cols, FEAT
            )
    grad_blocks = jnp.sum(feat_grad.reshape(block_rows, block_cols, NF, BS * BS) * own_slopes, axis=2)
    near_grad = to_cells(grad_blocks)
    framed = wide_widths[BS - 1 : BS + height + 1, BS - 1 : BS + columns + 1]
    grad_tv = variation(
        framed,
        lax.axis_index("px") * height,
        lax.axis_index("py") * columns,
        total_rows,
        total_cols,
    )
    return (far_field, near_grad + tv_weight * grad_tv)


def solution(mesh):
    return jax.shard_map(
        per_device,
        mesh=mesh,
        in_specs=(P("px", "py"), P("px", "py", None), P(), P(("px", "py"), None, None, None)),
        out_specs=(P(("px", "py"), None, None, None), P("px", "py")),
        check_vma=False,
    )
```

```python
import math

import jax
import jax.numpy as jnp
from jax import lax
from jax.sharding import PartitionSpec as P

BS = 8
NF = 4
NW = 8
NK = 512
FEAT = 256
OUTS = 1024


tv_weight = 0.5
tv_floor = 0.01


def with_halo(block, sides, width):
    for axis, dim in sides:
        count = lax.axis_size(axis)
        forward = [(i, i + 1) for i in range(count - 1)]
        backward = [(target, source) for source, target in forward]
        low = lax.ppermute(
            lax.slice_in_dim(block, block.shape[dim] - width, None, axis=dim), axis, forward
        )
        high = lax.ppermute(lax.slice_in_dim(block, 0, width, axis=dim), axis, backward)
        block = jnp.concatenate([low, block, high], axis=dim)
    return block


def chebyshev(normed, levels):
    values, slopes = ([], [])
    before = jnp.ones_like(normed)
    current = normed
    slope_before = jnp.zeros_like(normed)
    slope_now = jnp.ones_like(normed)
    for level in range(levels):
        values.append(current)
        slopes.append(slope_now)
        follow = 2.0 * normed * current - before
        slope_follow = 2.0 * current + 2.0 * normed * slope_now - slope_before
        before, current, slope_before, slope_now = (current, follow, slope_now, slope_follow)
    return (jnp.stack(values, 1), jnp.stack(slopes, 1))


def cell_blocks(planes, block_side):
    height, layers, columns = planes.shape
    shaped = planes.reshape(
        height // block_side, block_side, layers, columns // block_side, block_side
    )
    return shaped.transpose(0, 3, 1, 2, 4).reshape(
        height // block_side, columns // block_side, block_side * layers * block_side
    )


def block_cells(blocks, block_side, layers):
    block_rows, block_cols, unused = blocks.shape
    shaped = blocks.reshape(block_rows, block_cols, block_side, layers, block_side)
    return shaped.transpose(0, 2, 3, 1, 4).reshape(
        block_rows * block_side, layers, block_cols * block_side
    )


def field_rows(blocks, block_side, wave_count):
    block_rows, block_cols, unused = blocks.shape
    shaped = blocks.reshape(block_rows, block_cols, block_side, wave_count, 2 * block_side)
    return shaped.transpose(0, 2, 3, 1, 4).reshape(
        block_rows * block_side * wave_count, block_cols * 2 * block_side
    )


def rows_field(row_flat, block_side, wave_count):
    row_count, unused = row_flat.shape
    height = row_count // wave_count
    block_cols = unused // (2 * block_side)
    shaped = row_flat.reshape(
        height // block_side, block_side, wave_count, block_cols, 2 * block_side
    )
    return shaped.transpose(0, 3, 1, 2, 4).reshape(
        height // block_side, block_cols, block_side * wave_count * 2 * block_side
    )


def phase_table(first_col, col_count, total_cols):
    places = first_col + jnp.arange(col_count, dtype=jnp.int32)
    orders = jnp.arange(NK, dtype=jnp.int32) - NK // 2
    phase_turns = places[:, None] * orders[None, :] % total_cols
    angles = phase_turns.astype(jnp.float32) * (2.0 * math.pi / total_cols)
    cosine = jnp.cos(angles)
    sine_part = jnp.sin(angles)
    phase_rows = jnp.stack(
        [jnp.stack([cosine, -sine_part], 1), jnp.stack([sine_part, cosine], 1)], 1
    )
    phase_rows = phase_rows.astype(jnp.bfloat16).reshape(col_count // BS, BS, 2, 2 * NK)
    return phase_rows.transpose(0, 2, 1, 3).reshape(2 * col_count, 2 * NK)


def variation(framed, row_first, col_first, total_rows, total_cols):
    height = framed.shape[0] - 2
    columns = framed.shape[1] - 2
    step_down = framed[1:, :-1] - framed[:-1, :-1]
    step_right = framed[:-1, 1:] - framed[:-1, :-1]
    row_at = row_first - 1 + jnp.arange(height + 1, dtype=jnp.int32)
    col_at = col_first - 1 + jnp.arange(columns + 1, dtype=jnp.int32)
    step_down = jnp.where(((row_at >= 0) & (row_at < total_rows - 1))[:, None], step_down, 0.0)
    step_right = jnp.where(((col_at >= 0) & (col_at < total_cols - 1))[None, :], step_right, 0.0)
    magnitude = jnp.sqrt(step_down * step_down + step_right * step_right + tv_floor)
    flow_down = step_down / magnitude
    flow_right = step_right / magnitude
    return -(flow_down + flow_right)[1:, 1:] + flow_down[:-1, 1:] + flow_right[1:, :-1]


def lane_perm():
    rows = lax.broadcasted_iota(jnp.int32, (OUTS, OUTS), 0)
    cols = lax.broadcasted_iota(jnp.int32, (OUTS, OUTS), 1)
    inner = NW * BS
    hit = (rows // (2 * BS) == cols % inner) & (rows % (2 * BS) == cols // inner)
    return hit.astype(jnp.bfloat16)


def dft_table(total_cols):
    kk = jnp.arange(NK, dtype=jnp.int32) - NK // 2
    low = 8 * BS
    high = total_cols // low
    a = jnp.arange(high, dtype=jnp.int32)
    b = jnp.arange(low, dtype=jnp.int32)
    scale = 2.0 * math.pi / total_cols
    ta = ((a[:, None] * low * kk[None, :]) % total_cols).astype(jnp.float32) * scale
    tb = ((b[:, None] * kk[None, :]) % total_cols).astype(jnp.float32) * scale
    ca, sa = jnp.cos(ta), jnp.sin(ta)
    cb, sb = jnp.cos(tb), jnp.sin(tb)
    cb = cb.reshape(BS, BS, NK).transpose(1, 0, 2)
    sb = sb.reshape(BS, BS, NK).transpose(1, 0, 2)
    cos_v = ca[None, :, None, :] * cb[:, None, :, :] - sa[None, :, None, :] * sb[:, None, :, :]
    sin_v = sa[None, :, None, :] * cb[:, None, :, :] + ca[None, :, None, :] * sb[:, None, :, :]
    cos_v = cos_v.reshape(BS, total_cols // BS, NK)
    sin_v = sin_v.reshape(BS, total_cols // BS, NK)
    return jnp.concatenate([cos_v, sin_v], axis=-1).astype(jnp.bfloat16)


def to_blocks(cells):
    rows, cols = cells.shape
    shaped = cells.reshape(rows // BS, BS, cols // BS, BS).transpose(0, 2, 1, 3)
    return shaped.reshape(rows // BS, cols // BS, BS * BS)


def to_cells(blocks):
    rows, cols, unused = blocks.shape
    shaped = blocks.reshape(rows, cols, BS, BS).transpose(0, 2, 1, 3)
    return shaped.reshape(rows * BS, cols * BS)


def chebyshev_terms(normed, levels):
    values, slopes = ([], [])
    before = jnp.ones_like(normed)
    current = normed
    slope_before = jnp.zeros_like(normed)
    slope_now = jnp.ones_like(normed)
    for level in range(levels):
        values.append(current)
        slopes.append(slope_now)
        follow = 2.0 * normed * current - before
        slope_follow = 2.0 * current + 2.0 * normed * slope_now - slope_before
        before, current, slope_before, slope_now = (current, follow, slope_now, slope_follow)
    return values, slopes


def per_device(widths, couplings, surrogate, target_far):
    height, columns = widths.shape
    block_rows = height // BS
    block_cols = columns // BS
    groups = lax.axis_size("py")
    total_cols = columns * groups
    total_rows = height * lax.axis_size("px")
    wide_widths = with_halo(widths, (("px", 0), ("py", 1)), BS)
    wide_flags = with_halo(couplings.astype(jnp.bfloat16), (("px", 0), ("py", 1)), 1)
    values, slopes = chebyshev_terms(lax.optimization_barrier(to_blocks(wide_widths)), NF)
    features = jnp.concatenate(values, axis=-1).astype(jnp.bfloat16)
    own_slopes = jnp.stack([s[1 : block_rows + 1, 1 : block_cols + 1] for s in slopes], axis=2)
    new_rows = lax.broadcasted_iota(jnp.int32, (FEAT, FEAT), 0)
    old_rows = lax.broadcasted_iota(jnp.int32, (FEAT, FEAT), 1)
    same_f = new_rows // (BS * BS) == (old_rows // BS) % NF
    same_i = (new_rows // BS) % BS == old_rows // (NF * BS)
    same_j = new_rows % BS == old_rows % BS
    row_perm = (same_f & same_i & same_j).astype(jnp.bfloat16)
    sur = jnp.einsum(
        "ab,obn->oan", row_perm, surrogate, preferred_element_type=jnp.float32
    ).astype(jnp.bfloat16)
    wide_cols = block_cols + 2
    cells = (block_rows + 2) * wide_cols
    flat = jnp.pad(features.reshape(cells, FEAT), ((1, 1), (0, 0)))
    flat_flags = jnp.pad(wide_flags.reshape(cells, 9), ((1, 1), (0, 0)))
    span = block_rows * wide_cols
    pieces = []
    for row_step in range(3):
        for col_step in range(3):
            offset = row_step * 3 + col_step
            first = (2 - row_step) * wide_cols + (2 - col_step)
            pieces.append(
                flat[first : first + span] * flat_flags[first : first + span, offset : offset + 1]
            )
    stacked = jnp.concatenate(pieces, axis=-1)
    near_field = jnp.dot(
        stacked, sur.reshape(9 * FEAT, OUTS), preferred_element_type=jnp.float32
    ).astype(jnp.bfloat16)
    near_field = near_field.reshape(block_rows, wide_cols, OUTS)[:, 1 : block_cols + 1]
    perm = lane_perm()
    near_perm = jnp.dot(
        near_field.reshape(block_rows * block_cols, OUTS), perm, preferred_element_type=jnp.float32
    ).astype(jnp.bfloat16)
    near_perm = near_perm.reshape(block_rows, block_cols, OUTS)
    own_rows = lax.all_to_all(near_perm, "py", 0, 1, tiled=True)
    own_bx = own_rows.shape[0]
    all_by = own_rows.shape[1]
    table = dft_table(total_cols)
    norm_scale = 1.0 / math.sqrt(total_cols)
    lhs = own_rows.reshape(own_bx, all_by, 2, BS, NW * BS)
    parts = jnp.einsum("bYpji,jYq->bpiq", lhs, table, preferred_element_type=jnp.float32)
    real = parts[:, 0, :, :NK] + parts[:, 1, :, NK:]
    imag = parts[:, 1, :, :NK] - parts[:, 0, :, NK:]
    far_field = (jnp.stack([real, imag], axis=2) * norm_scale).reshape(own_bx * BS, NW, 2, NK)
    far_miss = (far_field - target_far.astype(jnp.float32)).astype(jnp.bfloat16)
    miss = far_miss.reshape(own_bx, NW * BS, 2, NK)
    miss_re = miss[:, :, 0]
    miss_im = miss[:, :, 1]
    rhs = jnp.stack(
        [
            jnp.concatenate([miss_re, -miss_im], axis=-1),
            jnp.concatenate([miss_im, miss_re], axis=-1),
        ],
        axis=1,
    )
    adj_flat = jnp.einsum("bpiq,jYq->bYpji", rhs, table, preferred_element_type=jnp.float32)
    adj_perm = (adj_flat * norm_scale).astype(jnp.bfloat16).reshape(own_bx, all_by, OUTS)
    adj_pad = jnp.pad(adj_perm, ((0, 0), (1, 1), (0, 0)))
    windows = jnp.stack(
        [adj_pad[:, d * block_cols : d * block_cols + wide_cols] for d in range(groups)]
    )
    adj_back = lax.all_to_all(windows, "py", 0, 0, tiled=True)
    adj_blocks = jnp.einsum(
        "bc,rc->br", adj_back.reshape(block_rows * wide_cols, OUTS), perm,
        preferred_element_type=jnp.float32,
    ).astype(jnp.bfloat16).reshape(block_rows, wide_cols, OUTS)
    wide_adj = with_halo(adj_blocks, (("px", 0),), 1)
    feat_grad = jnp.zeros((block_rows, block_cols, FEAT), jnp.float32)
    for row_step in range(3):
        for col_step in range(3):
            offset = row_step * 3 + col_step
            targets_at = wide_adj[
                row_step : row_step + block_rows, col_step : col_step + block_cols
            ]
            product = jnp.dot(
                targets_at.reshape(block_rows * block_cols, OUTS),
                sur[offset].T,
                preferred_element_type=jnp.float32,
            )
            flags = couplings[:, :, offset].astype(jnp.float32)
            feat_grad = feat_grad + flags[:, :, None] * product.reshape(
                block_rows, block_cols, FEAT
            )
    grad_blocks = jnp.sum(feat_grad.reshape(block_rows, block_cols, NF, BS * BS) * own_slopes, axis=2)
    near_grad = to_cells(grad_blocks)
    framed = wide_widths[BS - 1 : BS + height + 1, BS - 1 : BS + columns + 1]
    grad_tv = variation(
        framed,
        lax.axis_index("px") * height,
        lax.axis_index("py") * columns,
        total_rows,
        total_cols,
    )
    return (far_field, near_grad + tv_weight * grad_tv)


def solution(mesh):
    return jax.shard_map(
        per_device,
        mesh=mesh,
        in_specs=(P("px", "py"), P("px", "py", None), P(), P(("px", "py"), None, None, None)),
        out_specs=(P(("px", "py"), None, None, None), P("px", "py")),
        check_vma=False,
    )
```

```python
import math

import jax
import jax.numpy as jnp
from jax import lax
from jax.sharding import PartitionSpec as P

BS = 8
NF = 4
NW = 8
NK = 512
FEAT = 256
OUTS = 1024


tv_weight = 0.5
tv_floor = 0.01


def with_halo(block, sides, width):
    for axis, dim in sides:
        count = lax.axis_size(axis)
        forward = [(i, i + 1) for i in range(count - 1)]
        backward = [(target, source) for source, target in forward]
        low = lax.ppermute(
            lax.slice_in_dim(block, block.shape[dim] - width, None, axis=dim), axis, forward
        )
        high = lax.ppermute(lax.slice_in_dim(block, 0, width, axis=dim), axis, backward)
        block = jnp.concatenate([low, block, high], axis=dim)
    return block


def chebyshev(normed, levels):
    values, slopes = ([], [])
    before = jnp.ones_like(normed)
    current = normed
    slope_before = jnp.zeros_like(normed)
    slope_now = jnp.ones_like(normed)
    for level in range(levels):
        values.append(current)
        slopes.append(slope_now)
        follow = 2.0 * normed * current - before
        slope_follow = 2.0 * current + 2.0 * normed * slope_now - slope_before
        before, current, slope_before, slope_now = (current, follow, slope_now, slope_follow)
    return (jnp.stack(values, 1), jnp.stack(slopes, 1))


def cell_blocks(planes, block_side):
    height, layers, columns = planes.shape
    shaped = planes.reshape(
        height // block_side, block_side, layers, columns // block_side, block_side
    )
    return shaped.transpose(0, 3, 1, 2, 4).reshape(
        height // block_side, columns // block_side, block_side * layers * block_side
    )


def block_cells(blocks, block_side, layers):
    block_rows, block_cols, unused = blocks.shape
    shaped = blocks.reshape(block_rows, block_cols, block_side, layers, block_side)
    return shaped.transpose(0, 2, 3, 1, 4).reshape(
        block_rows * block_side, layers, block_cols * block_side
    )


def field_rows(blocks, block_side, wave_count):
    block_rows, block_cols, unused = blocks.shape
    shaped = blocks.reshape(block_rows, block_cols, block_side, wave_count, 2 * block_side)
    return shaped.transpose(0, 2, 3, 1, 4).reshape(
        block_rows * block_side * wave_count, block_cols * 2 * block_side
    )


def rows_field(row_flat, block_side, wave_count):
    row_count, unused = row_flat.shape
    height = row_count // wave_count
    block_cols = unused // (2 * block_side)
    shaped = row_flat.reshape(
        height // block_side, block_side, wave_count, block_cols, 2 * block_side
    )
    return shaped.transpose(0, 3, 1, 2, 4).reshape(
        height // block_side, block_cols, block_side * wave_count * 2 * block_side
    )


def phase_table(first_col, col_count, total_cols):
    places = first_col + jnp.arange(col_count, dtype=jnp.int32)
    orders = jnp.arange(NK, dtype=jnp.int32) - NK // 2
    phase_turns = places[:, None] * orders[None, :] % total_cols
    angles = phase_turns.astype(jnp.float32) * (2.0 * math.pi / total_cols)
    cosine = jnp.cos(angles)
    sine_part = jnp.sin(angles)
    phase_rows = jnp.stack(
        [jnp.stack([cosine, -sine_part], 1), jnp.stack([sine_part, cosine], 1)], 1
    )
    phase_rows = phase_rows.astype(jnp.bfloat16).reshape(col_count // BS, BS, 2, 2 * NK)
    return phase_rows.transpose(0, 2, 1, 3).reshape(2 * col_count, 2 * NK)


def variation(framed, row_first, col_first, total_rows, total_cols):
    height = framed.shape[0] - 2
    columns = framed.shape[1] - 2
    step_down = framed[1:, :-1] - framed[:-1, :-1]
    step_right = framed[:-1, 1:] - framed[:-1, :-1]
    row_at = row_first - 1 + jnp.arange(height + 1, dtype=jnp.int32)
    col_at = col_first - 1 + jnp.arange(columns + 1, dtype=jnp.int32)
    step_down = jnp.where(((row_at >= 0) & (row_at < total_rows - 1))[:, None], step_down, 0.0)
    step_right = jnp.where(((col_at >= 0) & (col_at < total_cols - 1))[None, :], step_right, 0.0)
    magnitude = jnp.sqrt(step_down * step_down + step_right * step_right + tv_floor)
    flow_down = step_down / magnitude
    flow_right = step_right / magnitude
    return -(flow_down + flow_right)[1:, 1:] + flow_down[:-1, 1:] + flow_right[1:, :-1]


def lane_perm():
    rows = lax.broadcasted_iota(jnp.int32, (OUTS, OUTS), 0)
    cols = lax.broadcasted_iota(jnp.int32, (OUTS, OUTS), 1)
    inner = NW * BS
    hit = (rows // (2 * BS) == cols % inner) & (rows % (2 * BS) == cols // inner)
    return hit.astype(jnp.bfloat16)


def dft_table(total_cols):
    kk = jnp.arange(NK, dtype=jnp.int32) - NK // 2
    low = 8 * BS
    high = total_cols // low
    a = jnp.arange(high, dtype=jnp.int32)
    b = jnp.arange(low, dtype=jnp.int32)
    scale = 2.0 * math.pi / total_cols
    ta = ((a[:, None] * low * kk[None, :]) % total_cols).astype(jnp.float32) * scale
    tb = ((b[:, None] * kk[None, :]) % total_cols).astype(jnp.float32) * scale
    ca, sa = jnp.cos(ta), jnp.sin(ta)
    cb, sb = jnp.cos(tb), jnp.sin(tb)
    cb = cb.reshape(BS, BS, NK).transpose(1, 0, 2)
    sb = sb.reshape(BS, BS, NK).transpose(1, 0, 2)
    cos_v = ca[None, :, None, :] * cb[:, None, :, :] - sa[None, :, None, :] * sb[:, None, :, :]
    sin_v = sa[None, :, None, :] * cb[:, None, :, :] + ca[None, :, None, :] * sb[:, None, :, :]
    cos_v = cos_v.reshape(BS, total_cols // BS, NK)
    sin_v = sin_v.reshape(BS, total_cols // BS, NK)
    return jnp.concatenate([cos_v, sin_v], axis=-1).astype(jnp.bfloat16)


def to_blocks(cells):
    rows, cols = cells.shape
    shaped = cells.reshape(rows // BS, BS, cols // BS, BS).transpose(0, 2, 1, 3)
    return shaped.reshape(rows // BS, cols // BS, BS * BS)


def to_cells(blocks):
    rows, cols, unused = blocks.shape
    shaped = blocks.reshape(rows, cols, BS, BS).transpose(0, 2, 1, 3)
    return shaped.reshape(rows * BS, cols * BS)


def chebyshev_terms(normed, levels):
    values, slopes = ([], [])
    before = jnp.ones_like(normed)
    current = normed
    slope_before = jnp.zeros_like(normed)
    slope_now = jnp.ones_like(normed)
    for level in range(levels):
        values.append(current)
        slopes.append(slope_now)
        follow = 2.0 * normed * current - before
        slope_follow = 2.0 * current + 2.0 * normed * slope_now - slope_before
        before, current, slope_before, slope_now = (current, follow, slope_now, slope_follow)
    return values, slopes


def per_device(widths, couplings, surrogate, target_far):
    height, columns = widths.shape
    block_rows = height // BS
    block_cols = columns // BS
    groups = lax.axis_size("py")
    devices = lax.axis_size("px") * groups
    total_cols = columns * groups
    total_rows = height * lax.axis_size("px")
    wide_widths = with_halo(widths, (("px", 0), ("py", 1)), BS)
    wide_flags = with_halo(couplings.astype(jnp.bfloat16), (("px", 0), ("py", 1)), 1)
    width_blocks = lax.optimization_barrier(to_blocks(wide_widths))
    values, unused = chebyshev_terms(width_blocks, NF)
    features = jnp.concatenate(values, axis=-1).astype(jnp.bfloat16)
    sur = surrogate.reshape(9, BS, NF, BS, OUTS).transpose(0, 2, 1, 3, 4).reshape(9, FEAT, OUTS)
    perm = lane_perm()
    sur = jnp.einsum("ofc,cd->ofd", sur, perm, preferred_element_type=jnp.float32).astype(
        jnp.bfloat16
    )
    wide_cols = block_cols + 2
    cells = (block_rows + 2) * wide_cols
    flat = jnp.pad(features.reshape(cells, FEAT), ((1, 1), (0, 0)))
    flat_flags = jnp.pad(wide_flags.reshape(cells, 9), ((1, 1), (0, 0)))
    span = block_rows * wide_cols
    pieces = []
    for row_step in range(3):
        for col_step in range(3):
            offset = row_step * 3 + col_step
            first = (2 - row_step) * wide_cols + (2 - col_step)
            pieces.append(
                flat[first : first + span] * flat_flags[first : first + span, offset : offset + 1]
            )
    stacked = jnp.concatenate(pieces, axis=-1)
    near_perm = jnp.dot(
        stacked, sur.reshape(9 * FEAT, OUTS), preferred_element_type=jnp.float32
    ).astype(jnp.bfloat16)
    near_perm = near_perm.reshape(block_rows, wide_cols, OUTS)[:, 1 : block_cols + 1]
    own_rows = lax.all_to_all(near_perm, "py", 0, 1, tiled=True)
    side = jnp.concatenate(
        [width_blocks[1:-1, 1:-1], couplings.astype(jnp.float32)], axis=-1
    )
    side_rows = lax.all_to_all(side, "py", 0, 1, tiled=True)
    own_bx = own_rows.shape[0]
    all_by = own_rows.shape[1]
    table = dft_table(total_cols)
    norm_scale = 1.0 / math.sqrt(total_cols)
    lhs = own_rows.reshape(own_bx, all_by, 2, BS, NW * BS)
    parts = jnp.einsum("bYpji,jYq->bpiq", lhs, table, preferred_element_type=jnp.float32)
    real = parts[:, 0, :, :NK] + parts[:, 1, :, NK:]
    imag = parts[:, 1, :, :NK] - parts[:, 0, :, NK:]
    far_field = (jnp.stack([real, imag], axis=2) * norm_scale).reshape(own_bx * BS, NW, 2, NK)
    far_miss = (far_field - target_far.astype(jnp.float32)).astype(jnp.bfloat16)
    down = [(i, i + 1) for i in range(devices - 1)]
    up = [(i + 1, i) for i in range(devices - 1)]
    above = lax.ppermute(far_miss[BS:], ("px", "py"), down)
    below = lax.ppermute(far_miss[:BS], ("px", "py"), up)
    rows4 = own_bx + 2
    miss = jnp.concatenate([above, far_miss, below]).reshape(rows4, NW * BS, 2, NK)
    miss_re = miss[:, :, 0]
    miss_im = miss[:, :, 1]
    rhs = jnp.stack(
        [
            jnp.concatenate([miss_re, -miss_im], axis=-1),
            jnp.concatenate([miss_im, miss_re], axis=-1),
        ],
        axis=1,
    )
    adj_flat = jnp.einsum("bpiq,jYq->bYpji", rhs, table, preferred_element_type=jnp.float32)
    adj = (adj_flat * norm_scale).astype(jnp.bfloat16).reshape(rows4, all_by, OUTS)
    wide_adj = jnp.pad(adj, ((0, 0), (1, 1), (0, 0)))
    own_flags = side_rows[:, :, BS * BS :]
    feat_grad = jnp.zeros((own_bx, all_by, FEAT), jnp.float32)
    for row_step in range(3):
        for col_step in range(3):
            offset = row_step * 3 + col_step
            targets_at = wide_adj[row_step : row_step + own_bx, col_step : col_step + all_by]
            product = jnp.dot(
                targets_at.reshape(own_bx * all_by, OUTS),
                sur[offset].T,
                preferred_element_type=jnp.float32,
            )
            flags = own_flags[:, :, offset]
            feat_grad = feat_grad + flags[:, :, None] * product.reshape(own_bx, all_by, FEAT)
    unused, slopes = chebyshev_terms(side_rows[:, :, : BS * BS], NF)
    grad_rows = feat_grad[:, :, : BS * BS] * slopes[0]
    for level in range(1, NF):
        grad_rows = grad_rows + feat_grad[:, :, level * BS * BS : (level + 1) * BS * BS] * slopes[level]
    grad_blocks = lax.all_to_all(grad_rows, "py", 1, 0, tiled=True)
    near_grad = to_cells(grad_blocks)
    framed = wide_widths[BS - 1 : BS + height + 1, BS - 1 : BS + columns + 1]
    grad_tv = variation(
        framed,
        lax.axis_index("px") * height,
        lax.axis_index("py") * columns,
        total_rows,
        total_cols,
    )
    return (far_field, near_grad + tv_weight * grad_tv)


def solution(mesh):
    return jax.shard_map(
        per_device,
        mesh=mesh,
        in_specs=(P("px", "py"), P("px", "py", None), P(), P(("px", "py"), None, None, None)),
        out_specs=(P(("px", "py"), None, None, None), P("px", "py")),
        check_vma=False,
    )
```

```python
import math

import jax
import jax.numpy as jnp
from jax import lax
from jax.sharding import PartitionSpec as P

BS = 8
NF = 4
NW = 8
NK = 512
FEAT = 256
OUTS = 1024


tv_weight = 0.5
tv_floor = 0.01


def with_halo(block, sides, width):
    for axis, dim in sides:
        count = lax.axis_size(axis)
        forward = [(i, i + 1) for i in range(count - 1)]
        backward = [(target, source) for source, target in forward]
        low = lax.ppermute(
            lax.slice_in_dim(block, block.shape[dim] - width, None, axis=dim), axis, forward
        )
        high = lax.ppermute(lax.slice_in_dim(block, 0, width, axis=dim), axis, backward)
        block = jnp.concatenate([low, block, high], axis=dim)
    return block


def chebyshev(normed, levels):
    values, slopes = ([], [])
    before = jnp.ones_like(normed)
    current = normed
    slope_before = jnp.zeros_like(normed)
    slope_now = jnp.ones_like(normed)
    for level in range(levels):
        values.append(current)
        slopes.append(slope_now)
        follow = 2.0 * normed * current - before
        slope_follow = 2.0 * current + 2.0 * normed * slope_now - slope_before
        before, current, slope_before, slope_now = (current, follow, slope_now, slope_follow)
    return (jnp.stack(values, 1), jnp.stack(slopes, 1))


def cell_blocks(planes, block_side):
    height, layers, columns = planes.shape
    shaped = planes.reshape(
        height // block_side, block_side, layers, columns // block_side, block_side
    )
    return shaped.transpose(0, 3, 1, 2, 4).reshape(
        height // block_side, columns // block_side, block_side * layers * block_side
    )


def block_cells(blocks, block_side, layers):
    block_rows, block_cols, unused = blocks.shape
    shaped = blocks.reshape(block_rows, block_cols, block_side, layers, block_side)
    return shaped.transpose(0, 2, 3, 1, 4).reshape(
        block_rows * block_side, layers, block_cols * block_side
    )


def field_rows(blocks, block_side, wave_count):
    block_rows, block_cols, unused = blocks.shape
    shaped = blocks.reshape(block_rows, block_cols, block_side, wave_count, 2 * block_side)
    return shaped.transpose(0, 2, 3, 1, 4).reshape(
        block_rows * block_side * wave_count, block_cols * 2 * block_side
    )


def rows_field(row_flat, block_side, wave_count):
    row_count, unused = row_flat.shape
    height = row_count // wave_count
    block_cols = unused // (2 * block_side)
    shaped = row_flat.reshape(
        height // block_side, block_side, wave_count, block_cols, 2 * block_side
    )
    return shaped.transpose(0, 3, 1, 2, 4).reshape(
        height // block_side, block_cols, block_side * wave_count * 2 * block_side
    )


def phase_table(first_col, col_count, total_cols):
    places = first_col + jnp.arange(col_count, dtype=jnp.int32)
    orders = jnp.arange(NK, dtype=jnp.int32) - NK // 2
    phase_turns = places[:, None] * orders[None, :] % total_cols
    angles = phase_turns.astype(jnp.float32) * (2.0 * math.pi / total_cols)
    cosine = jnp.cos(angles)
    sine_part = jnp.sin(angles)
    phase_rows = jnp.stack(
        [jnp.stack([cosine, -sine_part], 1), jnp.stack([sine_part, cosine], 1)], 1
    )
    phase_rows = phase_rows.astype(jnp.bfloat16).reshape(col_count // BS, BS, 2, 2 * NK)
    return phase_rows.transpose(0, 2, 1, 3).reshape(2 * col_count, 2 * NK)


def variation(framed, row_first, col_first, total_rows, total_cols):
    height = framed.shape[0] - 2
    columns = framed.shape[1] - 2
    step_down = framed[1:, :-1] - framed[:-1, :-1]
    step_right = framed[:-1, 1:] - framed[:-1, :-1]
    row_at = row_first - 1 + jnp.arange(height + 1, dtype=jnp.int32)
    col_at = col_first - 1 + jnp.arange(columns + 1, dtype=jnp.int32)
    step_down = jnp.where(((row_at >= 0) & (row_at < total_rows - 1))[:, None], step_down, 0.0)
    step_right = jnp.where(((col_at >= 0) & (col_at < total_cols - 1))[None, :], step_right, 0.0)
    magnitude = jnp.sqrt(step_down * step_down + step_right * step_right + tv_floor)
    flow_down = step_down / magnitude
    flow_right = step_right / magnitude
    return -(flow_down + flow_right)[1:, 1:] + flow_down[:-1, 1:] + flow_right[1:, :-1]


def lane_perm():
    rows = lax.broadcasted_iota(jnp.int32, (OUTS, OUTS), 0)
    cols = lax.broadcasted_iota(jnp.int32, (OUTS, OUTS), 1)
    inner = NW * BS
    hit = (rows // (2 * BS) == cols % inner) & (rows % (2 * BS) == cols // inner)
    return hit.astype(jnp.bfloat16)


def dft_table(total_cols):
    kk = jnp.arange(NK, dtype=jnp.int32) - NK // 2
    low = 8 * BS
    high = total_cols // low
    a = jnp.arange(high, dtype=jnp.int32)
    b = jnp.arange(low, dtype=jnp.int32)
    scale = 2.0 * math.pi / total_cols
    ta = ((a[:, None] * low * kk[None, :]) % total_cols).astype(jnp.float32) * scale
    tb = ((b[:, None] * kk[None, :]) % total_cols).astype(jnp.float32) * scale
    ca, sa = jnp.cos(ta), jnp.sin(ta)
    cb, sb = jnp.cos(tb), jnp.sin(tb)
    cb = cb.reshape(BS, BS, NK).transpose(1, 0, 2)
    sb = sb.reshape(BS, BS, NK).transpose(1, 0, 2)
    cos_v = ca[None, :, None, :] * cb[:, None, :, :] - sa[None, :, None, :] * sb[:, None, :, :]
    sin_v = sa[None, :, None, :] * cb[:, None, :, :] + ca[None, :, None, :] * sb[:, None, :, :]
    cos_v = cos_v.reshape(BS, total_cols // BS, NK)
    sin_v = sin_v.reshape(BS, total_cols // BS, NK)
    return jnp.concatenate([cos_v, sin_v], axis=-1).astype(jnp.bfloat16)


def to_blocks(cells):
    rows, cols = cells.shape
    shaped = cells.reshape(rows // BS, BS, cols // BS, BS).transpose(0, 2, 1, 3)
    return shaped.reshape(rows // BS, cols // BS, BS * BS)


def to_cells(blocks):
    rows, cols, unused = blocks.shape
    shaped = blocks.reshape(rows, cols, BS, BS).transpose(0, 2, 1, 3)
    return shaped.reshape(rows * BS, cols * BS)


def chebyshev_terms(normed, levels):
    values, slopes = ([], [])
    before = jnp.ones_like(normed)
    current = normed
    slope_before = jnp.zeros_like(normed)
    slope_now = jnp.ones_like(normed)
    for level in range(levels):
        values.append(current)
        slopes.append(slope_now)
        follow = 2.0 * normed * current - before
        slope_follow = 2.0 * current + 2.0 * normed * slope_now - slope_before
        before, current, slope_before, slope_now = (current, follow, slope_now, slope_follow)
    return values, slopes


def strip(cells, flags, total_cols, all_by):
    flag_rows = -(-all_by * 9 // total_cols)
    packed = jnp.pad(flags.reshape(-1), (0, flag_rows * total_cols - all_by * 9))
    return jnp.concatenate([cells, packed.reshape(flag_rows, total_cols)])


def unstrip(edge, all_by):
    return edge[:BS], edge[BS:].reshape(-1)[: all_by * 9].reshape(all_by, 9)


def per_device(widths, couplings, surrogate, target_far):
    height, columns = widths.shape
    groups = lax.axis_size("py")
    devices = lax.axis_size("px") * groups
    total_cols = columns * groups
    total_rows = height * lax.axis_size("px")
    rows = height // groups
    own_bx = rows // BS
    all_by = total_cols // BS
    block_cols = columns // BS
    place = lax.axis_index("px") * groups + lax.axis_index("py")
    flag_vals = own_bx * block_cols * 9
    flag_rows = -(-flag_vals // columns)
    packed_flags = jnp.pad(
        couplings.astype(jnp.float32).reshape(groups, flag_vals),
        ((0, 0), (0, flag_rows * columns - flag_vals)),
    ).reshape(groups, flag_rows, columns)
    packed = jnp.concatenate([widths.reshape(groups, rows, columns), packed_flags], axis=1)
    got = lax.all_to_all(
        packed.reshape(groups * (rows + flag_rows), columns), "py", 0, 1, tiled=True
    )
    own_w = got[:rows]
    got_flags = got[rows:].reshape(flag_rows, groups, columns).transpose(1, 0, 2)
    got_flags = got_flags.reshape(groups, flag_rows * columns)[:, :flag_vals]
    own_flags = got_flags.reshape(groups, own_bx, block_cols, 9).transpose(1, 0, 2, 3)
    own_flags = own_flags.reshape(own_bx, all_by, 9)
    down = [(i, i + 1) for i in range(devices - 1)]
    up = [(i + 1, i) for i in range(devices - 1)]
    above = lax.ppermute(
        strip(own_w[rows - BS :], own_flags[own_bx - 1], total_cols, all_by), ("px", "py"), down
    )
    below = lax.ppermute(strip(own_w[:BS], own_flags[0], total_cols, all_by), ("px", "py"), up)
    w_above, f_above = unstrip(above, all_by)
    w_below, f_below = unstrip(below, all_by)
    wide_w = jnp.concatenate([w_above, own_w, w_below])
    wide_flags = jnp.concatenate([f_above[None], own_flags, f_below[None]])
    rows4 = own_bx + 2
    width_blocks = lax.optimization_barrier(to_blocks(wide_w))
    values, unused = chebyshev_terms(width_blocks, NF)
    features = jnp.concatenate(values, axis=-1).astype(jnp.bfloat16)
    sur = surrogate.reshape(9, BS, NF, BS, OUTS).transpose(0, 2, 1, 3, 4).reshape(9, FEAT, OUTS)
    perm = lane_perm()
    sur = jnp.einsum("ofc,cd->ofd", sur, perm, preferred_element_type=jnp.float32).astype(
        jnp.bfloat16
    )
    wide_cols = all_by + 2
    cells = rows4 * wide_cols
    features = jnp.pad(features, ((0, 0), (1, 1), (0, 0)))
    flags16 = jnp.pad(wide_flags.astype(jnp.bfloat16), ((0, 0), (1, 1), (0, 0)))
    flat = jnp.pad(features.reshape(cells, FEAT), ((1, 1), (0, 0)))
    flat_flags = jnp.pad(flags16.reshape(cells, 9), ((1, 1), (0, 0)))
    span = own_bx * wide_cols
    pieces = []
    for row_step in range(3):
        for col_step in range(3):
            offset = row_step * 3 + col_step
            first = (2 - row_step) * wide_cols + (2 - col_step)
            pieces.append(
                flat[first : first + span] * flat_flags[first : first + span, offset : offset + 1]
            )
    stacked = jnp.concatenate(pieces, axis=-1)
    near_perm = jnp.dot(
        stacked, sur.reshape(9 * FEAT, OUTS), preferred_element_type=jnp.float32
    ).astype(jnp.bfloat16)
    own_rows = near_perm.reshape(own_bx, wide_cols, OUTS)[:, 1 : all_by + 1]
    table = dft_table(total_cols)
    norm_scale = 1.0 / math.sqrt(total_cols)
    lhs = own_rows.reshape(own_bx, all_by, 2, BS, NW * BS)
    parts = jnp.einsum("bYpji,jYq->bpiq", lhs, table, preferred_element_type=jnp.float32)
    real = parts[:, 0, :, :NK] + parts[:, 1, :, NK:]
    imag = parts[:, 1, :, :NK] - parts[:, 0, :, NK:]
    far_field = (jnp.stack([real, imag], axis=2) * norm_scale).reshape(own_bx * BS, NW, 2, NK)
    far_miss = (far_field - target_far.astype(jnp.float32)).astype(jnp.bfloat16)
    miss_above = lax.ppermute(far_miss[BS:], ("px", "py"), down)
    miss_below = lax.ppermute(far_miss[:BS], ("px", "py"), up)
    miss = jnp.concatenate([miss_above, far_miss, miss_below]).reshape(rows4, NW * BS, 2, NK)
    miss_re = miss[:, :, 0]
    miss_im = miss[:, :, 1]
    rhs = jnp.stack(
        [
            jnp.concatenate([miss_re, -miss_im], axis=-1),
            jnp.concatenate([miss_im, miss_re], axis=-1),
        ],
        axis=1,
    )
    adj_flat = jnp.einsum("bpiq,jYq->bYpji", rhs, table, preferred_element_type=jnp.float32)
    adj = (adj_flat * norm_scale).astype(jnp.bfloat16).reshape(rows4, all_by, OUTS)
    wide_adj = jnp.pad(adj, ((0, 0), (1, 1), (0, 0)))
    feat_grad = jnp.zeros((own_bx, all_by, FEAT), jnp.float32)
    for row_step in range(3):
        for col_step in range(3):
            offset = row_step * 3 + col_step
            targets_at = wide_adj[row_step : row_step + own_bx, col_step : col_step + all_by]
            product = jnp.dot(
                targets_at.reshape(own_bx * all_by, OUTS),
                sur[offset].T,
                preferred_element_type=jnp.float32,
            )
            flags = own_flags[:, :, offset]
            feat_grad = feat_grad + flags[:, :, None] * product.reshape(own_bx, all_by, FEAT)
    unused, slopes = chebyshev_terms(width_blocks[1 : own_bx + 1], NF)
    grad_rows = feat_grad[:, :, : BS * BS] * slopes[0]
    for level in range(1, NF):
        grad_rows = grad_rows + feat_grad[:, :, level * BS * BS : (level + 1) * BS * BS] * slopes[level]
    near_grad = to_cells(grad_rows)
    framed = jnp.pad(wide_w[BS - 1 : BS + rows + 1], ((0, 0), (1, 1)))
    grad_tv = variation(framed, place * rows, 0, total_rows, total_cols)
    row_grad = near_grad + tv_weight * grad_tv
    width_grad = lax.all_to_all(row_grad, "py", 1, 0, tiled=True)
    return (far_field, width_grad)


def solution(mesh):
    return jax.shard_map(
        per_device,
        mesh=mesh,
        in_specs=(P("px", "py"), P("px", "py", None), P(), P(("px", "py"), None, None, None)),
        out_specs=(P(("px", "py"), None, None, None), P("px", "py")),
        check_vma=False,
    )
```

```python
import math

import jax
import jax.numpy as jnp
from jax import lax
from jax.sharding import PartitionSpec as P

BS = 8
NF = 4
NW = 8
NK = 512
FEAT = 256
OUTS = 1024


tv_weight = 0.5
tv_floor = 0.01


def with_halo(block, sides, width):
    for axis, dim in sides:
        count = lax.axis_size(axis)
        forward = [(i, i + 1) for i in range(count - 1)]
        backward = [(target, source) for source, target in forward]
        low = lax.ppermute(
            lax.slice_in_dim(block, block.shape[dim] - width, None, axis=dim), axis, forward
        )
        high = lax.ppermute(lax.slice_in_dim(block, 0, width, axis=dim), axis, backward)
        block = jnp.concatenate([low, block, high], axis=dim)
    return block


def chebyshev(normed, levels):
    values, slopes = ([], [])
    before = jnp.ones_like(normed)
    current = normed
    slope_before = jnp.zeros_like(normed)
    slope_now = jnp.ones_like(normed)
    for level in range(levels):
        values.append(current)
        slopes.append(slope_now)
        follow = 2.0 * normed * current - before
        slope_follow = 2.0 * current + 2.0 * normed * slope_now - slope_before
        before, current, slope_before, slope_now = (current, follow, slope_now, slope_follow)
    return (jnp.stack(values, 1), jnp.stack(slopes, 1))


def cell_blocks(planes, block_side):
    height, layers, columns = planes.shape
    shaped = planes.reshape(
        height // block_side, block_side, layers, columns // block_side, block_side
    )
    return shaped.transpose(0, 3, 1, 2, 4).reshape(
        height // block_side, columns // block_side, block_side * layers * block_side
    )


def block_cells(blocks, block_side, layers):
    block_rows, block_cols, unused = blocks.shape
    shaped = blocks.reshape(block_rows, block_cols, block_side, layers, block_side)
    return shaped.transpose(0, 2, 3, 1, 4).reshape(
        block_rows * block_side, layers, block_cols * block_side
    )


def field_rows(blocks, block_side, wave_count):
    block_rows, block_cols, unused = blocks.shape
    shaped = blocks.reshape(block_rows, block_cols, block_side, wave_count, 2 * block_side)
    return shaped.transpose(0, 2, 3, 1, 4).reshape(
        block_rows * block_side * wave_count, block_cols * 2 * block_side
    )


def rows_field(row_flat, block_side, wave_count):
    row_count, unused = row_flat.shape
    height = row_count // wave_count
    block_cols = unused // (2 * block_side)
    shaped = row_flat.reshape(
        height // block_side, block_side, wave_count, block_cols, 2 * block_side
    )
    return shaped.transpose(0, 3, 1, 2, 4).reshape(
        height // block_side, block_cols, block_side * wave_count * 2 * block_side
    )


def phase_table(first_col, col_count, total_cols):
    places = first_col + jnp.arange(col_count, dtype=jnp.int32)
    orders = jnp.arange(NK, dtype=jnp.int32) - NK // 2
    phase_turns = places[:, None] * orders[None, :] % total_cols
    angles = phase_turns.astype(jnp.float32) * (2.0 * math.pi / total_cols)
    cosine = jnp.cos(angles)
    sine_part = jnp.sin(angles)
    phase_rows = jnp.stack(
        [jnp.stack([cosine, -sine_part], 1), jnp.stack([sine_part, cosine], 1)], 1
    )
    phase_rows = phase_rows.astype(jnp.bfloat16).reshape(col_count // BS, BS, 2, 2 * NK)
    return phase_rows.transpose(0, 2, 1, 3).reshape(2 * col_count, 2 * NK)


def variation(framed, row_first, col_first, total_rows, total_cols):
    height = framed.shape[0] - 2
    columns = framed.shape[1] - 2
    step_down = framed[1:, :-1] - framed[:-1, :-1]
    step_right = framed[:-1, 1:] - framed[:-1, :-1]
    row_at = row_first - 1 + jnp.arange(height + 1, dtype=jnp.int32)
    col_at = col_first - 1 + jnp.arange(columns + 1, dtype=jnp.int32)
    step_down = jnp.where(((row_at >= 0) & (row_at < total_rows - 1))[:, None], step_down, 0.0)
    step_right = jnp.where(((col_at >= 0) & (col_at < total_cols - 1))[None, :], step_right, 0.0)
    magnitude = jnp.sqrt(step_down * step_down + step_right * step_right + tv_floor)
    flow_down = step_down / magnitude
    flow_right = step_right / magnitude
    return -(flow_down + flow_right)[1:, 1:] + flow_down[:-1, 1:] + flow_right[1:, :-1]


def lane_perm():
    rows = lax.broadcasted_iota(jnp.int32, (OUTS, OUTS), 0)
    cols = lax.broadcasted_iota(jnp.int32, (OUTS, OUTS), 1)
    inner = NW * BS
    hit = (rows // (2 * BS) == cols % inner) & (rows % (2 * BS) == cols // inner)
    return hit.astype(jnp.bfloat16)


def dft_table(total_cols):
    kk = jnp.arange(NK, dtype=jnp.int32) - NK // 2
    low = 8 * BS
    high = total_cols // low
    a = jnp.arange(high, dtype=jnp.int32)
    b = jnp.arange(low, dtype=jnp.int32)
    scale = 2.0 * math.pi / total_cols
    ta = ((a[:, None] * low * kk[None, :]) % total_cols).astype(jnp.float32) * scale
    tb = ((b[:, None] * kk[None, :]) % total_cols).astype(jnp.float32) * scale
    ca, sa = jnp.cos(ta), jnp.sin(ta)
    cb, sb = jnp.cos(tb), jnp.sin(tb)
    cb = cb.reshape(BS, BS, NK).transpose(1, 0, 2)
    sb = sb.reshape(BS, BS, NK).transpose(1, 0, 2)
    cos_v = ca[None, :, None, :] * cb[:, None, :, :] - sa[None, :, None, :] * sb[:, None, :, :]
    sin_v = sa[None, :, None, :] * cb[:, None, :, :] + ca[None, :, None, :] * sb[:, None, :, :]
    cos_v = cos_v.reshape(BS, total_cols // BS, NK)
    sin_v = sin_v.reshape(BS, total_cols // BS, NK)
    return jnp.concatenate([cos_v, sin_v], axis=-1).astype(jnp.bfloat16)


def to_blocks(cells):
    rows, cols = cells.shape
    shaped = cells.reshape(rows // BS, BS, cols // BS, BS).transpose(0, 2, 1, 3)
    return shaped.reshape(rows // BS, cols // BS, BS * BS)


def to_cells(blocks):
    rows, cols, unused = blocks.shape
    shaped = blocks.reshape(rows, cols, BS, BS).transpose(0, 2, 1, 3)
    return shaped.reshape(rows * BS, cols * BS)


def chebyshev_terms(normed, levels):
    values, slopes = ([], [])
    before = jnp.ones_like(normed)
    current = normed
    slope_before = jnp.zeros_like(normed)
    slope_now = jnp.ones_like(normed)
    for level in range(levels):
        values.append(current)
        slopes.append(slope_now)
        follow = 2.0 * normed * current - before
        slope_follow = 2.0 * current + 2.0 * normed * slope_now - slope_before
        before, current, slope_before, slope_now = (current, follow, slope_now, slope_follow)
    return values, slopes


def strip(cells, flags, total_cols, all_by):
    flag_rows = -(-all_by * 9 // total_cols)
    packed = jnp.pad(flags.reshape(-1), (0, flag_rows * total_cols - all_by * 9))
    return jnp.concatenate([cells, packed.reshape(flag_rows, total_cols)])


def unstrip(edge, all_by):
    return edge[:BS], edge[BS:].reshape(-1)[: all_by * 9].reshape(all_by, 9)


def per_device(widths, couplings, surrogate, target_far):
    height, columns = widths.shape
    groups = lax.axis_size("py")
    devices = lax.axis_size("px") * groups
    total_cols = columns * groups
    total_rows = height * lax.axis_size("px")
    rows = height // groups
    own_bx = rows // BS
    all_by = total_cols // BS
    block_cols = columns // BS
    place = lax.axis_index("px") * groups + lax.axis_index("py")
    down = [(i, i + 1) for i in range(devices - 1)]
    up = [(i + 1, i) for i in range(devices - 1)]
    block_rows = height // BS
    flag_vals = block_cols * 9
    flag_rows = -(-flag_vals // columns)
    packed_flags = jnp.pad(
        couplings.astype(jnp.float32).reshape(block_rows, flag_vals),
        ((0, 0), (0, flag_rows * columns - flag_vals)),
    ).reshape(block_rows, flag_rows, columns)
    count = lax.axis_size("px")
    forward = [(i, i + 1) for i in range(count - 1)]
    backward = [(i + 1, i) for i in range(count - 1)]
    low = lax.ppermute(
        jnp.concatenate([widths[height - BS :], packed_flags[block_rows - 1]]), "px", forward
    )
    high = lax.ppermute(jnp.concatenate([widths[:BS], packed_flags[0]]), "px", backward)
    tall_w = jnp.concatenate([low[:BS], widths, high[:BS]])
    tall_f = jnp.concatenate([low[BS:][None], packed_flags, high[BS:][None]])
    win_w = jnp.concatenate(
        [tall_w[:height].reshape(groups, rows, columns), tall_w[2 * BS :].reshape(groups, rows, columns)],
        axis=1,
    )
    win_f = jnp.concatenate(
        [
            tall_f[:block_rows].reshape(groups, own_bx * flag_rows, columns),
            tall_f[2:].reshape(groups, own_bx * flag_rows, columns),
        ],
        axis=1,
    )
    packed = jnp.concatenate([win_w, win_f], axis=1)
    depth = packed.shape[1]
    got = lax.all_to_all(packed.reshape(groups * depth, columns), "py", 0, 1, tiled=True)
    rows4 = own_bx + 2
    wide_w = got[: 2 * rows]
    got_flags = got[2 * rows :].reshape(rows4, flag_rows, groups, columns).transpose(0, 2, 1, 3)
    got_flags = got_flags.reshape(rows4, groups, flag_rows * columns)[:, :, :flag_vals]
    wide_flags = got_flags.reshape(rows4, all_by, 9)
    own_flags = wide_flags[1 : own_bx + 1]
    width_blocks = lax.optimization_barrier(to_blocks(wide_w))
    values, unused = chebyshev_terms(width_blocks, NF)
    features = jnp.concatenate(values, axis=-1).astype(jnp.bfloat16)
    sur = surrogate.reshape(9, BS, NF, BS, OUTS).transpose(0, 2, 1, 3, 4).reshape(9, FEAT, OUTS)
    perm = lane_perm()
    sur = jnp.einsum("ofc,cd->ofd", sur, perm, preferred_element_type=jnp.float32).astype(
        jnp.bfloat16
    )
    wide_cols = all_by + 2
    cells = rows4 * wide_cols
    features = jnp.pad(features, ((0, 0), (1, 1), (0, 0)))
    flags16 = jnp.pad(wide_flags.astype(jnp.bfloat16), ((0, 0), (1, 1), (0, 0)))
    flat = jnp.pad(features.reshape(cells, FEAT), ((1, 1), (0, 0)))
    flat_flags = jnp.pad(flags16.reshape(cells, 9), ((1, 1), (0, 0)))
    span = own_bx * wide_cols
    pieces = []
    for row_step in range(3):
        for col_step in range(3):
            offset = row_step * 3 + col_step
            first = (2 - row_step) * wide_cols + (2 - col_step)
            pieces.append(
                flat[first : first + span] * flat_flags[first : first + span, offset : offset + 1]
            )
    stacked = jnp.concatenate(pieces, axis=-1)
    near_perm = jnp.dot(
        stacked, sur.reshape(9 * FEAT, OUTS), preferred_element_type=jnp.float32
    ).astype(jnp.bfloat16)
    own_rows = near_perm.reshape(own_bx, wide_cols, OUTS)[:, 1 : all_by + 1]
    table = dft_table(total_cols)
    norm_scale = 1.0 / math.sqrt(total_cols)
    lhs = own_rows.reshape(own_bx, all_by, 2, BS, NW * BS)
    parts = jnp.einsum("bYpji,jYq->bpiq", lhs, table, preferred_element_type=jnp.float32)
    real = parts[:, 0, :, :NK] + parts[:, 1, :, NK:]
    imag = parts[:, 1, :, :NK] - parts[:, 0, :, NK:]
    far_field = (jnp.stack([real, imag], axis=2) * norm_scale).reshape(own_bx * BS, NW, 2, NK)
    far_miss = (far_field - target_far.astype(jnp.float32)).astype(jnp.bfloat16)
    miss_above = lax.ppermute(far_miss[BS:], ("px", "py"), down)
    miss_below = lax.ppermute(far_miss[:BS], ("px", "py"), up)
    miss = jnp.concatenate([miss_above, far_miss, miss_below]).reshape(rows4, NW * BS, 2, NK)
    miss_re = miss[:, :, 0]
    miss_im = miss[:, :, 1]
    rhs = jnp.stack(
        [
            jnp.concatenate([miss_re, -miss_im], axis=-1),
            jnp.concatenate([miss_im, miss_re], axis=-1),
        ],
        axis=1,
    )
    adj_flat = jnp.einsum("bpiq,jYq->bYpji", rhs, table, preferred_element_type=jnp.float32)
    adj = (adj_flat * norm_scale).astype(jnp.bfloat16).reshape(rows4, all_by, OUTS)
    wide_adj = jnp.pad(adj, ((0, 0), (1, 1), (0, 0)))
    feat_grad = jnp.zeros((own_bx, all_by, FEAT), jnp.float32)
    for row_step in range(3):
        for col_step in range(3):
            offset = row_step * 3 + col_step
            targets_at = wide_adj[row_step : row_step + own_bx, col_step : col_step + all_by]
            product = jnp.dot(
                targets_at.reshape(own_bx * all_by, OUTS),
                sur[offset].T,
                preferred_element_type=jnp.float32,
            )
            flags = own_flags[:, :, offset]
            feat_grad = feat_grad + flags[:, :, None] * product.reshape(own_bx, all_by, FEAT)
    unused, slopes = chebyshev_terms(width_blocks[1 : own_bx + 1], NF)
    grad_rows = feat_grad[:, :, : BS * BS] * slopes[0]
    for level in range(1, NF):
        grad_rows = grad_rows + feat_grad[:, :, level * BS * BS : (level + 1) * BS * BS] * slopes[level]
    near_grad = to_cells(grad_rows)
    framed = jnp.pad(wide_w[BS - 1 : BS + rows + 1], ((0, 0), (1, 1)))
    grad_tv = variation(framed, place * rows, 0, total_rows, total_cols)
    row_grad = near_grad + tv_weight * grad_tv
    width_grad = lax.all_to_all(row_grad, "py", 1, 0, tiled=True)
    return (far_field, width_grad)


def solution(mesh):
    return jax.shard_map(
        per_device,
        mesh=mesh,
        in_specs=(P("px", "py"), P("px", "py", None), P(), P(("px", "py"), None, None, None)),
        out_specs=(P(("px", "py"), None, None, None), P("px", "py")),
        check_vma=False,
    )
```

```python
import math

import jax
import jax.numpy as jnp
from jax import lax
from jax.sharding import PartitionSpec as P

BS = 8
NF = 4
NW = 8
NK = 512
FEAT = 256
OUTS = 1024


tv_weight = 0.5
tv_floor = 0.01


def with_halo(block, sides, width):
    for axis, dim in sides:
        count = lax.axis_size(axis)
        forward = [(i, i + 1) for i in range(count - 1)]
        backward = [(target, source) for source, target in forward]
        low = lax.ppermute(
            lax.slice_in_dim(block, block.shape[dim] - width, None, axis=dim), axis, forward
        )
        high = lax.ppermute(lax.slice_in_dim(block, 0, width, axis=dim), axis, backward)
        block = jnp.concatenate([low, block, high], axis=dim)
    return block


def chebyshev(normed, levels):
    values, slopes = ([], [])
    before = jnp.ones_like(normed)
    current = normed
    slope_before = jnp.zeros_like(normed)
    slope_now = jnp.ones_like(normed)
    for level in range(levels):
        values.append(current)
        slopes.append(slope_now)
        follow = 2.0 * normed * current - before
        slope_follow = 2.0 * current + 2.0 * normed * slope_now - slope_before
        before, current, slope_before, slope_now = (current, follow, slope_now, slope_follow)
    return (jnp.stack(values, 1), jnp.stack(slopes, 1))


def cell_blocks(planes, block_side):
    height, layers, columns = planes.shape
    shaped = planes.reshape(
        height // block_side, block_side, layers, columns // block_side, block_side
    )
    return shaped.transpose(0, 3, 1, 2, 4).reshape(
        height // block_side, columns // block_side, block_side * layers * block_side
    )


def block_cells(blocks, block_side, layers):
    block_rows, block_cols, unused = blocks.shape
    shaped = blocks.reshape(block_rows, block_cols, block_side, layers, block_side)
    return shaped.transpose(0, 2, 3, 1, 4).reshape(
        block_rows * block_side, layers, block_cols * block_side
    )


def field_rows(blocks, block_side, wave_count):
    block_rows, block_cols, unused = blocks.shape
    shaped = blocks.reshape(block_rows, block_cols, block_side, wave_count, 2 * block_side)
    return shaped.transpose(0, 2, 3, 1, 4).reshape(
        block_rows * block_side * wave_count, block_cols * 2 * block_side
    )


def rows_field(row_flat, block_side, wave_count):
    row_count, unused = row_flat.shape
    height = row_count // wave_count
    block_cols = unused // (2 * block_side)
    shaped = row_flat.reshape(
        height // block_side, block_side, wave_count, block_cols, 2 * block_side
    )
    return shaped.transpose(0, 3, 1, 2, 4).reshape(
        height // block_side, block_cols, block_side * wave_count * 2 * block_side
    )


def phase_table(first_col, col_count, total_cols):
    places = first_col + jnp.arange(col_count, dtype=jnp.int32)
    orders = jnp.arange(NK, dtype=jnp.int32) - NK // 2
    phase_turns = places[:, None] * orders[None, :] % total_cols
    angles = phase_turns.astype(jnp.float32) * (2.0 * math.pi / total_cols)
    cosine = jnp.cos(angles)
    sine_part = jnp.sin(angles)
    phase_rows = jnp.stack(
        [jnp.stack([cosine, -sine_part], 1), jnp.stack([sine_part, cosine], 1)], 1
    )
    phase_rows = phase_rows.astype(jnp.bfloat16).reshape(col_count // BS, BS, 2, 2 * NK)
    return phase_rows.transpose(0, 2, 1, 3).reshape(2 * col_count, 2 * NK)


def variation(framed, row_first, col_first, total_rows, total_cols):
    height = framed.shape[0] - 2
    columns = framed.shape[1] - 2
    step_down = framed[1:, :-1] - framed[:-1, :-1]
    step_right = framed[:-1, 1:] - framed[:-1, :-1]
    row_at = row_first - 1 + jnp.arange(height + 1, dtype=jnp.int32)
    col_at = col_first - 1 + jnp.arange(columns + 1, dtype=jnp.int32)
    step_down = jnp.where(((row_at >= 0) & (row_at < total_rows - 1))[:, None], step_down, 0.0)
    step_right = jnp.where(((col_at >= 0) & (col_at < total_cols - 1))[None, :], step_right, 0.0)
    magnitude = jnp.sqrt(step_down * step_down + step_right * step_right + tv_floor)
    flow_down = step_down / magnitude
    flow_right = step_right / magnitude
    return -(flow_down + flow_right)[1:, 1:] + flow_down[:-1, 1:] + flow_right[1:, :-1]


def lane_perm():
    rows = lax.broadcasted_iota(jnp.int32, (OUTS, OUTS), 0)
    cols = lax.broadcasted_iota(jnp.int32, (OUTS, OUTS), 1)
    inner = NW * BS
    hit = (rows // (2 * BS) == cols % inner) & (rows % (2 * BS) == cols // inner)
    return hit.astype(jnp.bfloat16)


def dft_table(total_cols):
    kk = jnp.arange(NK, dtype=jnp.int32) - NK // 2
    low = 8 * BS
    high = total_cols // low
    a = jnp.arange(high, dtype=jnp.int32)
    b = jnp.arange(low, dtype=jnp.int32)
    scale = 2.0 * math.pi / total_cols
    ta = ((a[:, None] * low * kk[None, :]) % total_cols).astype(jnp.float32) * scale
    tb = ((b[:, None] * kk[None, :]) % total_cols).astype(jnp.float32) * scale
    ca, sa = jnp.cos(ta), jnp.sin(ta)
    cb, sb = jnp.cos(tb), jnp.sin(tb)
    cb = cb.reshape(BS, BS, NK).transpose(1, 0, 2)
    sb = sb.reshape(BS, BS, NK).transpose(1, 0, 2)
    cos_v = ca[None, :, None, :] * cb[:, None, :, :] - sa[None, :, None, :] * sb[:, None, :, :]
    sin_v = sa[None, :, None, :] * cb[:, None, :, :] + ca[None, :, None, :] * sb[:, None, :, :]
    cos_v = cos_v.reshape(BS, total_cols // BS, NK)
    sin_v = sin_v.reshape(BS, total_cols // BS, NK)
    return jnp.concatenate([cos_v, sin_v], axis=-1).astype(jnp.bfloat16)


def to_blocks(cells):
    rows, cols = cells.shape
    shaped = cells.reshape(rows // BS, BS, cols // BS, BS).transpose(0, 2, 1, 3)
    return shaped.reshape(rows // BS, cols // BS, BS * BS)


def to_cells(blocks):
    rows, cols, unused = blocks.shape
    shaped = blocks.reshape(rows, cols, BS, BS).transpose(0, 2, 1, 3)
    return shaped.reshape(rows * BS, cols * BS)


def chebyshev_terms(normed, levels):
    values, slopes = ([], [])
    before = jnp.ones_like(normed)
    current = normed
    slope_before = jnp.zeros_like(normed)
    slope_now = jnp.ones_like(normed)
    for level in range(levels):
        values.append(current)
        slopes.append(slope_now)
        follow = 2.0 * normed * current - before
        slope_follow = 2.0 * current + 2.0 * normed * slope_now - slope_before
        before, current, slope_before, slope_now = (current, follow, slope_now, slope_follow)
    return values, slopes


def strip(cells, flags, total_cols, all_by):
    flag_rows = -(-all_by * 9 // total_cols)
    packed = jnp.pad(flags.reshape(-1), (0, flag_rows * total_cols - all_by * 9))
    return jnp.concatenate([cells, packed.reshape(flag_rows, total_cols)])


def unstrip(edge, all_by):
    return edge[:BS], edge[BS:].reshape(-1)[: all_by * 9].reshape(all_by, 9)


def per_device(widths, couplings, surrogate, target_far):
    height, columns = widths.shape
    groups = lax.axis_size("py")
    devices = lax.axis_size("px") * groups
    total_cols = columns * groups
    total_rows = height * lax.axis_size("px")
    rows = height // groups
    own_bx = rows // BS
    all_by = total_cols // BS
    block_cols = columns // BS
    place = lax.axis_index("px") * groups + lax.axis_index("py")
    down = [(i, i + 1) for i in range(devices - 1)]
    up = [(i + 1, i) for i in range(devices - 1)]
    block_rows = height // BS
    flag_vals = block_cols * 9
    flag_rows = -(-flag_vals // columns)
    packed_flags = jnp.pad(
        couplings.astype(jnp.float32).reshape(block_rows, flag_vals),
        ((0, 0), (0, flag_rows * columns - flag_vals)),
    ).reshape(block_rows, flag_rows, columns)
    count = lax.axis_size("px")
    forward = [(i, i + 1) for i in range(count - 1)]
    backward = [(i + 1, i) for i in range(count - 1)]
    low = lax.ppermute(
        jnp.concatenate([widths[height - BS :], packed_flags[block_rows - 1]]), "px", forward
    )
    high = lax.ppermute(jnp.concatenate([widths[:BS], packed_flags[0]]), "px", backward)
    tall_w = jnp.concatenate([low[:BS], widths, high[:BS]])
    tall_f = jnp.concatenate([low[BS:][None], packed_flags, high[BS:][None]])
    win_w = jnp.concatenate(
        [tall_w[:height].reshape(groups, rows, columns), tall_w[2 * BS :].reshape(groups, rows, columns)],
        axis=1,
    )
    win_f = jnp.concatenate(
        [
            tall_f[:block_rows].reshape(groups, own_bx * flag_rows, columns),
            tall_f[2:].reshape(groups, own_bx * flag_rows, columns),
        ],
        axis=1,
    )
    packed = jnp.concatenate([win_w, win_f], axis=1)
    packed, surrogate = lax.optimization_barrier((packed, surrogate))
    depth = packed.shape[1]
    got = lax.all_to_all(packed.reshape(groups * depth, columns), "py", 0, 1, tiled=True)
    rows4 = own_bx + 2
    wide_w = got[: 2 * rows]
    got_flags = got[2 * rows :].reshape(rows4, flag_rows, groups, columns).transpose(0, 2, 1, 3)
    got_flags = got_flags.reshape(rows4, groups, flag_rows * columns)[:, :, :flag_vals]
    wide_flags = got_flags.reshape(rows4, all_by, 9)
    own_flags = wide_flags[1 : own_bx + 1]
    width_blocks = lax.optimization_barrier(to_blocks(wide_w))
    values, unused = chebyshev_terms(width_blocks, NF)
    features = jnp.concatenate(values, axis=-1).astype(jnp.bfloat16)
    sur = surrogate.reshape(9, BS, NF, BS, OUTS).transpose(0, 2, 1, 3, 4).reshape(9, FEAT, OUTS)
    perm = lane_perm()
    sur = jnp.einsum("ofc,cd->ofd", sur, perm, preferred_element_type=jnp.float32).astype(
        jnp.bfloat16
    )
    wide_cols = all_by + 2
    cells = rows4 * wide_cols
    features = jnp.pad(features, ((0, 0), (1, 1), (0, 0)))
    flags16 = jnp.pad(wide_flags.astype(jnp.bfloat16), ((0, 0), (1, 1), (0, 0)))
    flat = jnp.pad(features.reshape(cells, FEAT), ((1, 1), (0, 0)))
    flat_flags = jnp.pad(flags16.reshape(cells, 9), ((1, 1), (0, 0)))
    span = own_bx * wide_cols
    pieces = []
    for row_step in range(3):
        for col_step in range(3):
            offset = row_step * 3 + col_step
            first = (2 - row_step) * wide_cols + (2 - col_step)
            pieces.append(
                flat[first : first + span] * flat_flags[first : first + span, offset : offset + 1]
            )
    stacked = jnp.concatenate(pieces, axis=-1)
    near_perm = jnp.dot(
        stacked, sur.reshape(9 * FEAT, OUTS), preferred_element_type=jnp.float32
    ).astype(jnp.bfloat16)
    own_rows = near_perm.reshape(own_bx, wide_cols, OUTS)[:, 1 : all_by + 1]
    table = dft_table(total_cols)
    norm_scale = 1.0 / math.sqrt(total_cols)
    lhs = own_rows.reshape(own_bx, all_by, 2, BS, NW * BS)
    parts = jnp.einsum("bYpji,jYq->bpiq", lhs, table, preferred_element_type=jnp.float32)
    real = parts[:, 0, :, :NK] + parts[:, 1, :, NK:]
    imag = parts[:, 1, :, :NK] - parts[:, 0, :, NK:]
    far_field = (jnp.stack([real, imag], axis=2) * norm_scale).reshape(own_bx * BS, NW, 2, NK)
    far_miss = (far_field - target_far.astype(jnp.float32)).astype(jnp.bfloat16)
    miss_above = lax.ppermute(far_miss[BS:], ("px", "py"), down)
    miss_below = lax.ppermute(far_miss[:BS], ("px", "py"), up)
    miss = jnp.concatenate([miss_above, far_miss, miss_below]).reshape(rows4, NW * BS, 2, NK)
    miss_re = miss[:, :, 0]
    miss_im = miss[:, :, 1]
    rhs = jnp.stack(
        [
            jnp.concatenate([miss_re, -miss_im], axis=-1),
            jnp.concatenate([miss_im, miss_re], axis=-1),
        ],
        axis=1,
    )
    adj_flat = jnp.einsum("bpiq,jYq->bYpji", rhs, table, preferred_element_type=jnp.float32)
    adj = (adj_flat * norm_scale).astype(jnp.bfloat16).reshape(rows4, all_by, OUTS)
    wide_adj = jnp.pad(adj, ((0, 0), (1, 1), (0, 0)))
    feat_grad = jnp.zeros((own_bx, all_by, FEAT), jnp.float32)
    for row_step in range(3):
        for col_step in range(3):
            offset = row_step * 3 + col_step
            targets_at = wide_adj[row_step : row_step + own_bx, col_step : col_step + all_by]
            product = jnp.dot(
                targets_at.reshape(own_bx * all_by, OUTS),
                sur[offset].T,
                preferred_element_type=jnp.float32,
            )
            flags = own_flags[:, :, offset]
            feat_grad = feat_grad + flags[:, :, None] * product.reshape(own_bx, all_by, FEAT)
    unused, slopes = chebyshev_terms(width_blocks[1 : own_bx + 1], NF)
    grad_rows = feat_grad[:, :, : BS * BS] * slopes[0]
    for level in range(1, NF):
        grad_rows = grad_rows + feat_grad[:, :, level * BS * BS : (level + 1) * BS * BS] * slopes[level]
    near_grad = to_cells(grad_rows)
    framed = jnp.pad(wide_w[BS - 1 : BS + rows + 1], ((0, 0), (1, 1)))
    grad_tv = variation(framed, place * rows, 0, total_rows, total_cols)
    row_grad = near_grad + tv_weight * grad_tv
    width_grad = lax.all_to_all(row_grad, "py", 1, 0, tiled=True)
    return (far_field, width_grad)


def solution(mesh):
    return jax.shard_map(
        per_device,
        mesh=mesh,
        in_specs=(P("px", "py"), P("px", "py", None), P(), P(("px", "py"), None, None, None)),
        out_specs=(P(("px", "py"), None, None, None), P("px", "py")),
        check_vma=False,
    )
```

```python
import math

import jax
import jax.numpy as jnp
from jax import lax
from jax.sharding import PartitionSpec as P

BS = 8
NF = 4
NW = 8
NK = 512
FEAT = 256
OUTS = 1024


tv_weight = 0.5
tv_floor = 0.01


def with_halo(block, sides, width):
    for axis, dim in sides:
        count = lax.axis_size(axis)
        forward = [(i, i + 1) for i in range(count - 1)]
        backward = [(target, source) for source, target in forward]
        low = lax.ppermute(
            lax.slice_in_dim(block, block.shape[dim] - width, None, axis=dim), axis, forward
        )
        high = lax.ppermute(lax.slice_in_dim(block, 0, width, axis=dim), axis, backward)
        block = jnp.concatenate([low, block, high], axis=dim)
    return block


def chebyshev(normed, levels):
    values, slopes = ([], [])
    before = jnp.ones_like(normed)
    current = normed
    slope_before = jnp.zeros_like(normed)
    slope_now = jnp.ones_like(normed)
    for level in range(levels):
        values.append(current)
        slopes.append(slope_now)
        follow = 2.0 * normed * current - before
        slope_follow = 2.0 * current + 2.0 * normed * slope_now - slope_before
        before, current, slope_before, slope_now = (current, follow, slope_now, slope_follow)
    return (jnp.stack(values, 1), jnp.stack(slopes, 1))


def cell_blocks(planes, block_side):
    height, layers, columns = planes.shape
    shaped = planes.reshape(
        height // block_side, block_side, layers, columns // block_side, block_side
    )
    return shaped.transpose(0, 3, 1, 2, 4).reshape(
        height // block_side, columns // block_side, block_side * layers * block_side
    )


def block_cells(blocks, block_side, layers):
    block_rows, block_cols, unused = blocks.shape
    shaped = blocks.reshape(block_rows, block_cols, block_side, layers, block_side)
    return shaped.transpose(0, 2, 3, 1, 4).reshape(
        block_rows * block_side, layers, block_cols * block_side
    )


def field_rows(blocks, block_side, wave_count):
    block_rows, block_cols, unused = blocks.shape
    shaped = blocks.reshape(block_rows, block_cols, block_side, wave_count, 2 * block_side)
    return shaped.transpose(0, 2, 3, 1, 4).reshape(
        block_rows * block_side * wave_count, block_cols * 2 * block_side
    )


def rows_field(row_flat, block_side, wave_count):
    row_count, unused = row_flat.shape
    height = row_count // wave_count
    block_cols = unused // (2 * block_side)
    shaped = row_flat.reshape(
        height // block_side, block_side, wave_count, block_cols, 2 * block_side
    )
    return shaped.transpose(0, 3, 1, 2, 4).reshape(
        height // block_side, block_cols, block_side * wave_count * 2 * block_side
    )


def phase_table(first_col, col_count, total_cols):
    places = first_col + jnp.arange(col_count, dtype=jnp.int32)
    orders = jnp.arange(NK, dtype=jnp.int32) - NK // 2
    phase_turns = places[:, None] * orders[None, :] % total_cols
    angles = phase_turns.astype(jnp.float32) * (2.0 * math.pi / total_cols)
    cosine = jnp.cos(angles)
    sine_part = jnp.sin(angles)
    phase_rows = jnp.stack(
        [jnp.stack([cosine, -sine_part], 1), jnp.stack([sine_part, cosine], 1)], 1
    )
    phase_rows = phase_rows.astype(jnp.bfloat16).reshape(col_count // BS, BS, 2, 2 * NK)
    return phase_rows.transpose(0, 2, 1, 3).reshape(2 * col_count, 2 * NK)


def variation(framed, row_first, col_first, total_rows, total_cols):
    height = framed.shape[0] - 2
    columns = framed.shape[1] - 2
    step_down = framed[1:, :-1] - framed[:-1, :-1]
    step_right = framed[:-1, 1:] - framed[:-1, :-1]
    row_at = row_first - 1 + jnp.arange(height + 1, dtype=jnp.int32)
    col_at = col_first - 1 + jnp.arange(columns + 1, dtype=jnp.int32)
    step_down = jnp.where(((row_at >= 0) & (row_at < total_rows - 1))[:, None], step_down, 0.0)
    step_right = jnp.where(((col_at >= 0) & (col_at < total_cols - 1))[None, :], step_right, 0.0)
    magnitude = jnp.sqrt(step_down * step_down + step_right * step_right + tv_floor)
    flow_down = step_down / magnitude
    flow_right = step_right / magnitude
    return -(flow_down + flow_right)[1:, 1:] + flow_down[:-1, 1:] + flow_right[1:, :-1]


def lane_perm():
    rows = lax.broadcasted_iota(jnp.int32, (OUTS, OUTS), 0)
    cols = lax.broadcasted_iota(jnp.int32, (OUTS, OUTS), 1)
    inner = NW * BS
    hit = (rows // (2 * BS) == cols % inner) & (rows % (2 * BS) == cols // inner)
    return hit.astype(jnp.bfloat16)


def dft_table(total_cols):
    kk = jnp.arange(NK, dtype=jnp.int32) - NK // 2
    low = 8 * BS
    high = total_cols // low
    a = jnp.arange(high, dtype=jnp.int32)
    b = jnp.arange(low, dtype=jnp.int32)
    scale = 2.0 * math.pi / total_cols
    ta = ((a[:, None] * low * kk[None, :]) % total_cols).astype(jnp.float32) * scale
    tb = ((b[:, None] * kk[None, :]) % total_cols).astype(jnp.float32) * scale
    ca, sa = jnp.cos(ta), jnp.sin(ta)
    cb, sb = jnp.cos(tb), jnp.sin(tb)
    cb = cb.reshape(BS, BS, NK).transpose(1, 0, 2)
    sb = sb.reshape(BS, BS, NK).transpose(1, 0, 2)
    cos_v = ca[None, :, None, :] * cb[:, None, :, :] - sa[None, :, None, :] * sb[:, None, :, :]
    sin_v = sa[None, :, None, :] * cb[:, None, :, :] + ca[None, :, None, :] * sb[:, None, :, :]
    cos_v = cos_v.reshape(BS, total_cols // BS, NK)
    sin_v = sin_v.reshape(BS, total_cols // BS, NK)
    return jnp.concatenate([cos_v, sin_v], axis=-1).astype(jnp.bfloat16)


def to_blocks(cells):
    rows, cols = cells.shape
    shaped = cells.reshape(rows // BS, BS, cols // BS, BS).transpose(0, 2, 1, 3)
    return shaped.reshape(rows // BS, cols // BS, BS * BS)


def to_cells(blocks):
    rows, cols, unused = blocks.shape
    shaped = blocks.reshape(rows, cols, BS, BS).transpose(0, 2, 1, 3)
    return shaped.reshape(rows * BS, cols * BS)


def chebyshev_terms(normed, levels):
    values, slopes = ([], [])
    before = jnp.ones_like(normed)
    current = normed
    slope_before = jnp.zeros_like(normed)
    slope_now = jnp.ones_like(normed)
    for level in range(levels):
        values.append(current)
        slopes.append(slope_now)
        follow = 2.0 * normed * current - before
        slope_follow = 2.0 * current + 2.0 * normed * slope_now - slope_before
        before, current, slope_before, slope_now = (current, follow, slope_now, slope_follow)
    return values, slopes


def strip(cells, flags, total_cols, all_by):
    flag_rows = -(-all_by * 9 // total_cols)
    packed = jnp.pad(flags.reshape(-1), (0, flag_rows * total_cols - all_by * 9))
    return jnp.concatenate([cells, packed.reshape(flag_rows, total_cols)])


def unstrip(edge, all_by):
    return edge[:BS], edge[BS:].reshape(-1)[: all_by * 9].reshape(all_by, 9)


def per_device(widths, couplings, surrogate, target_far):
    height, columns = widths.shape
    groups = lax.axis_size("py")
    devices = lax.axis_size("px") * groups
    total_cols = columns * groups
    total_rows = height * lax.axis_size("px")
    rows = height // groups
    own_bx = rows // BS
    all_by = total_cols // BS
    block_cols = columns // BS
    place = lax.axis_index("px") * groups + lax.axis_index("py")
    down = [(i, i + 1) for i in range(devices - 1)]
    up = [(i + 1, i) for i in range(devices - 1)]
    block_rows = height // BS
    flag_vals = block_cols * 9
    flag_rows = -(-flag_vals // columns)
    packed_flags = jnp.pad(
        couplings.astype(jnp.float32).reshape(block_rows, flag_vals),
        ((0, 0), (0, flag_rows * columns - flag_vals)),
    ).reshape(block_rows, flag_rows, columns)
    count = lax.axis_size("px")
    forward = [(i, i + 1) for i in range(count - 1)]
    backward = [(i + 1, i) for i in range(count - 1)]
    low = lax.ppermute(
        jnp.concatenate([widths[height - BS :], packed_flags[block_rows - 1]]), "px", forward
    )
    high = lax.ppermute(jnp.concatenate([widths[:BS], packed_flags[0]]), "px", backward)
    tall_w = jnp.concatenate([low[:BS], widths, high[:BS]])
    tall_f = jnp.concatenate([low[BS:][None], packed_flags, high[BS:][None]])
    win_w = jnp.concatenate(
        [tall_w[:height].reshape(groups, rows, columns), tall_w[2 * BS :].reshape(groups, rows, columns)],
        axis=1,
    )
    win_f = jnp.concatenate(
        [
            tall_f[:block_rows].reshape(groups, own_bx * flag_rows, columns),
            tall_f[2:].reshape(groups, own_bx * flag_rows, columns),
        ],
        axis=1,
    )
    packed = jnp.concatenate([win_w, win_f], axis=1)
    packed, surrogate = lax.optimization_barrier((packed, surrogate))
    depth = packed.shape[1]
    got = lax.all_to_all(packed.reshape(groups * depth, columns), "py", 0, 1, tiled=True)
    rows4 = own_bx + 2
    wide_w = got[: 2 * rows]
    got_flags = got[2 * rows :].reshape(rows4, flag_rows, groups, columns).transpose(0, 2, 1, 3)
    got_flags = got_flags.reshape(rows4, groups, flag_rows * columns)[:, :, :flag_vals]
    wide_flags = got_flags.reshape(rows4, all_by, 9)
    own_flags = wide_flags[1 : own_bx + 1]
    width_blocks = lax.optimization_barrier(to_blocks(wide_w))
    values, unused = chebyshev_terms(width_blocks, NF)
    features = jnp.concatenate(values, axis=-1).astype(jnp.bfloat16)
    sur = surrogate.reshape(9, BS, NF, BS, OUTS).transpose(0, 2, 1, 3, 4).reshape(9, FEAT, OUTS)
    perm = lane_perm()
    sur = jnp.einsum("ofc,cd->ofd", sur, perm, preferred_element_type=jnp.float32).astype(
        jnp.bfloat16
    )
    wide_cols = all_by + 2
    cells = rows4 * wide_cols
    features = jnp.pad(features, ((0, 0), (1, 1), (0, 0)))
    flags16 = jnp.pad(wide_flags.astype(jnp.bfloat16), ((0, 0), (1, 1), (0, 0)))
    flat = jnp.pad(features.reshape(cells, FEAT), ((1, 1), (0, 0)))
    flat_flags = jnp.pad(flags16.reshape(cells, 9), ((1, 1), (0, 0)))
    span = own_bx * wide_cols
    pieces = []
    for row_step in range(3):
        for col_step in range(3):
            offset = row_step * 3 + col_step
            first = (2 - row_step) * wide_cols + (2 - col_step)
            pieces.append(
                flat[first : first + span] * flat_flags[first : first + span, offset : offset + 1]
            )
    stacked = jnp.concatenate(pieces, axis=-1)
    near_perm = jnp.dot(
        stacked, sur.reshape(9 * FEAT, OUTS), preferred_element_type=jnp.float32
    ).astype(jnp.bfloat16)
    own_rows = near_perm.reshape(own_bx, wide_cols, OUTS)
    table = jnp.pad(dft_table(total_cols), ((0, 0), (1, 1), (0, 0)))
    norm_scale = 1.0 / math.sqrt(total_cols)
    lhs = own_rows.reshape(own_bx, wide_cols, 2, BS, NW * BS)
    parts = jnp.einsum("bYpji,jYq->bpiq", lhs, table, preferred_element_type=jnp.float32)
    real = parts[:, 0, :, :NK] + parts[:, 1, :, NK:]
    imag = parts[:, 1, :, :NK] - parts[:, 0, :, NK:]
    far_field = (jnp.stack([real, imag], axis=2) * norm_scale).reshape(own_bx * BS, NW, 2, NK)
    far_miss = (far_field - target_far.astype(jnp.float32)).astype(jnp.bfloat16)
    miss_above = lax.ppermute(far_miss[BS:], ("px", "py"), down)
    miss_below = lax.ppermute(far_miss[:BS], ("px", "py"), up)
    miss = jnp.concatenate([miss_above, far_miss, miss_below]).reshape(rows4, NW * BS, 2, NK)
    miss_re = miss[:, :, 0]
    miss_im = miss[:, :, 1]
    rhs = jnp.stack(
        [
            jnp.concatenate([miss_re, -miss_im], axis=-1),
            jnp.concatenate([miss_im, miss_re], axis=-1),
        ],
        axis=1,
    )
    adj_flat = jnp.einsum("bpiq,jYq->bYpji", rhs, table, preferred_element_type=jnp.float32)
    wide_adj = (adj_flat * norm_scale).astype(jnp.bfloat16).reshape(rows4, wide_cols, OUTS)
    feat_grad = jnp.zeros((own_bx, all_by, FEAT), jnp.float32)
    for row_step in range(3):
        for col_step in range(3):
            offset = row_step * 3 + col_step
            targets_at = wide_adj[row_step : row_step + own_bx, col_step : col_step + all_by]
            product = jnp.dot(
                targets_at.reshape(own_bx * all_by, OUTS),
                sur[offset].T,
                preferred_element_type=jnp.float32,
            )
            flags = own_flags[:, :, offset]
            feat_grad = feat_grad + flags[:, :, None] * product.reshape(own_bx, all_by, FEAT)
    unused, slopes = chebyshev_terms(width_blocks[1 : own_bx + 1], NF)
    grad_rows = feat_grad[:, :, : BS * BS] * slopes[0]
    for level in range(1, NF):
        grad_rows = grad_rows + feat_grad[:, :, level * BS * BS : (level + 1) * BS * BS] * slopes[level]
    near_grad = to_cells(grad_rows)
    framed = jnp.pad(wide_w[BS - 1 : BS + rows + 1], ((0, 0), (1, 1)))
    grad_tv = variation(framed, place * rows, 0, total_rows, total_cols)
    row_grad = near_grad + tv_weight * grad_tv
    width_grad = lax.all_to_all(row_grad, "py", 1, 0, tiled=True)
    return (far_field, width_grad)


def solution(mesh):
    return jax.shard_map(
        per_device,
        mesh=mesh,
        in_specs=(P("px", "py"), P("px", "py", None), P(), P(("px", "py"), None, None, None)),
        out_specs=(P(("px", "py"), None, None, None), P("px", "py")),
        check_vma=False,
    )
```

```python
import math

import jax
import jax.numpy as jnp
from jax import lax
from jax.sharding import PartitionSpec as P

BS = 8
NF = 4
NW = 8
NK = 512
FEAT = 256
OUTS = 1024


tv_weight = 0.5
tv_floor = 0.01


def with_halo(block, sides, width):
    for axis, dim in sides:
        count = lax.axis_size(axis)
        forward = [(i, i + 1) for i in range(count - 1)]
        backward = [(target, source) for source, target in forward]
        low = lax.ppermute(
            lax.slice_in_dim(block, block.shape[dim] - width, None, axis=dim), axis, forward
        )
        high = lax.ppermute(lax.slice_in_dim(block, 0, width, axis=dim), axis, backward)
        block = jnp.concatenate([low, block, high], axis=dim)
    return block


def chebyshev(normed, levels):
    values, slopes = ([], [])
    before = jnp.ones_like(normed)
    current = normed
    slope_before = jnp.zeros_like(normed)
    slope_now = jnp.ones_like(normed)
    for level in range(levels):
        values.append(current)
        slopes.append(slope_now)
        follow = 2.0 * normed * current - before
        slope_follow = 2.0 * current + 2.0 * normed * slope_now - slope_before
        before, current, slope_before, slope_now = (current, follow, slope_now, slope_follow)
    return (jnp.stack(values, 1), jnp.stack(slopes, 1))


def cell_blocks(planes, block_side):
    height, layers, columns = planes.shape
    shaped = planes.reshape(
        height // block_side, block_side, layers, columns // block_side, block_side
    )
    return shaped.transpose(0, 3, 1, 2, 4).reshape(
        height // block_side, columns // block_side, block_side * layers * block_side
    )


def block_cells(blocks, block_side, layers):
    block_rows, block_cols, unused = blocks.shape
    shaped = blocks.reshape(block_rows, block_cols, block_side, layers, block_side)
    return shaped.transpose(0, 2, 3, 1, 4).reshape(
        block_rows * block_side, layers, block_cols * block_side
    )


def field_rows(blocks, block_side, wave_count):
    block_rows, block_cols, unused = blocks.shape
    shaped = blocks.reshape(block_rows, block_cols, block_side, wave_count, 2 * block_side)
    return shaped.transpose(0, 2, 3, 1, 4).reshape(
        block_rows * block_side * wave_count, block_cols * 2 * block_side
    )


def rows_field(row_flat, block_side, wave_count):
    row_count, unused = row_flat.shape
    height = row_count // wave_count
    block_cols = unused // (2 * block_side)
    shaped = row_flat.reshape(
        height // block_side, block_side, wave_count, block_cols, 2 * block_side
    )
    return shaped.transpose(0, 3, 1, 2, 4).reshape(
        height // block_side, block_cols, block_side * wave_count * 2 * block_side
    )


def phase_table(first_col, col_count, total_cols):
    places = first_col + jnp.arange(col_count, dtype=jnp.int32)
    orders = jnp.arange(NK, dtype=jnp.int32) - NK // 2
    phase_turns = places[:, None] * orders[None, :] % total_cols
    angles = phase_turns.astype(jnp.float32) * (2.0 * math.pi / total_cols)
    cosine = jnp.cos(angles)
    sine_part = jnp.sin(angles)
    phase_rows = jnp.stack(
        [jnp.stack([cosine, -sine_part], 1), jnp.stack([sine_part, cosine], 1)], 1
    )
    phase_rows = phase_rows.astype(jnp.bfloat16).reshape(col_count // BS, BS, 2, 2 * NK)
    return phase_rows.transpose(0, 2, 1, 3).reshape(2 * col_count, 2 * NK)


def variation(framed, row_first, col_first, total_rows, total_cols):
    height = framed.shape[0] - 2
    columns = framed.shape[1] - 2
    step_down = framed[1:, :-1] - framed[:-1, :-1]
    step_right = framed[:-1, 1:] - framed[:-1, :-1]
    row_at = row_first - 1 + jnp.arange(height + 1, dtype=jnp.int32)
    col_at = col_first - 1 + jnp.arange(columns + 1, dtype=jnp.int32)
    step_down = jnp.where(((row_at >= 0) & (row_at < total_rows - 1))[:, None], step_down, 0.0)
    step_right = jnp.where(((col_at >= 0) & (col_at < total_cols - 1))[None, :], step_right, 0.0)
    magnitude = jnp.sqrt(step_down * step_down + step_right * step_right + tv_floor)
    flow_down = step_down / magnitude
    flow_right = step_right / magnitude
    return -(flow_down + flow_right)[1:, 1:] + flow_down[:-1, 1:] + flow_right[1:, :-1]


def lane_perm():
    rows = lax.broadcasted_iota(jnp.int32, (OUTS, OUTS), 0)
    cols = lax.broadcasted_iota(jnp.int32, (OUTS, OUTS), 1)
    inner = NW * BS
    hit = (rows // (2 * BS) == cols % inner) & (rows % (2 * BS) == cols // inner)
    return hit.astype(jnp.bfloat16)


def dft_table(total_cols):
    kk = jnp.arange(NK, dtype=jnp.int32) - NK // 2
    low = 8 * BS
    high = total_cols // low
    a = jnp.arange(high, dtype=jnp.int32)
    b = jnp.arange(low, dtype=jnp.int32)
    scale = 2.0 * math.pi / total_cols
    ta = ((a[:, None] * low * kk[None, :]) % total_cols).astype(jnp.float32) * scale
    tb = ((b[:, None] * kk[None, :]) % total_cols).astype(jnp.float32) * scale
    ca, sa = jnp.cos(ta), jnp.sin(ta)
    cb, sb = jnp.cos(tb), jnp.sin(tb)
    cb = cb.reshape(BS, BS, NK).transpose(1, 0, 2)
    sb = sb.reshape(BS, BS, NK).transpose(1, 0, 2)
    cos_v = ca[None, :, None, :] * cb[:, None, :, :] - sa[None, :, None, :] * sb[:, None, :, :]
    sin_v = sa[None, :, None, :] * cb[:, None, :, :] + ca[None, :, None, :] * sb[:, None, :, :]
    cos_v = cos_v.reshape(BS, total_cols // BS, NK)
    sin_v = sin_v.reshape(BS, total_cols // BS, NK)
    return jnp.concatenate([cos_v, sin_v], axis=-1).astype(jnp.bfloat16)


def to_blocks(cells):
    rows, cols = cells.shape
    shaped = cells.reshape(rows // BS, BS, cols // BS, BS).transpose(0, 2, 1, 3)
    return shaped.reshape(rows // BS, cols // BS, BS * BS)


def to_cells(blocks):
    rows, cols, unused = blocks.shape
    shaped = blocks.reshape(rows, cols, BS, BS).transpose(0, 2, 1, 3)
    return shaped.reshape(rows * BS, cols * BS)


def chebyshev_terms(normed, levels):
    values, slopes = ([], [])
    before = jnp.ones_like(normed)
    current = normed
    slope_before = jnp.zeros_like(normed)
    slope_now = jnp.ones_like(normed)
    for level in range(levels):
        values.append(current)
        slopes.append(slope_now)
        follow = 2.0 * normed * current - before
        slope_follow = 2.0 * current + 2.0 * normed * slope_now - slope_before
        before, current, slope_before, slope_now = (current, follow, slope_now, slope_follow)
    return values, slopes


def strip(cells, flags, total_cols, all_by):
    flag_rows = -(-all_by * 9 // total_cols)
    packed = jnp.pad(flags.reshape(-1), (0, flag_rows * total_cols - all_by * 9))
    return jnp.concatenate([cells, packed.reshape(flag_rows, total_cols)])


def unstrip(edge, all_by):
    return edge[:BS], edge[BS:].reshape(-1)[: all_by * 9].reshape(all_by, 9)


def per_device(widths, couplings, surrogate, target_far):
    height, columns = widths.shape
    groups = lax.axis_size("py")
    devices = lax.axis_size("px") * groups
    total_cols = columns * groups
    total_rows = height * lax.axis_size("px")
    rows = height // groups
    own_bx = rows // BS
    all_by = total_cols // BS
    block_cols = columns // BS
    place = lax.axis_index("px") * groups + lax.axis_index("py")
    down = [(i, i + 1) for i in range(devices - 1)]
    up = [(i + 1, i) for i in range(devices - 1)]
    block_rows = height // BS
    flag_vals = block_cols * 9
    flag_rows = -(-flag_vals // columns)
    packed_flags = jnp.pad(
        couplings.astype(jnp.float32).reshape(block_rows, flag_vals),
        ((0, 0), (0, flag_rows * columns - flag_vals)),
    ).reshape(block_rows, flag_rows, columns)
    count = lax.axis_size("px")
    forward = [(i, i + 1) for i in range(count - 1)]
    backward = [(i + 1, i) for i in range(count - 1)]
    low = lax.ppermute(
        jnp.concatenate([widths[height - BS :], packed_flags[block_rows - 1]]), "px", forward
    )
    high = lax.ppermute(jnp.concatenate([widths[:BS], packed_flags[0]]), "px", backward)
    tall_w = jnp.concatenate([low[:BS], widths, high[:BS]])
    tall_f = jnp.concatenate([low[BS:][None], packed_flags, high[BS:][None]])
    win_w = jnp.concatenate(
        [tall_w[:height].reshape(groups, rows, columns), tall_w[2 * BS :].reshape(groups, rows, columns)],
        axis=1,
    )
    win_f = jnp.concatenate(
        [
            tall_f[:block_rows].reshape(groups, own_bx * flag_rows, columns),
            tall_f[2:].reshape(groups, own_bx * flag_rows, columns),
        ],
        axis=1,
    )
    packed = jnp.concatenate([win_w, win_f], axis=1)
    packed, surrogate = lax.optimization_barrier((packed, surrogate))
    depth = packed.shape[1]
    got = lax.all_to_all(packed.reshape(groups * depth, columns), "py", 0, 1, tiled=True)
    rows4 = own_bx + 2
    wide_w = got[: 2 * rows]
    got_flags = got[2 * rows :].reshape(rows4, flag_rows, groups, columns).transpose(0, 2, 1, 3)
    got_flags = got_flags.reshape(rows4, groups, flag_rows * columns)[:, :, :flag_vals]
    wide_flags = got_flags.reshape(rows4, all_by, 9)
    own_flags = wide_flags[1 : own_bx + 1]
    width_blocks = lax.optimization_barrier(to_blocks(wide_w))
    values, unused = chebyshev_terms(width_blocks, NF)
    features = jnp.concatenate(values, axis=-1).astype(jnp.bfloat16)
    sur = surrogate.reshape(9, BS, NF, BS, OUTS).transpose(0, 2, 1, 3, 4).reshape(9, FEAT, OUTS)
    perm = lane_perm()
    sur = jnp.einsum("ofc,cd->ofd", sur, perm, preferred_element_type=jnp.float32).astype(
        jnp.bfloat16
    )
    wide_cols = -(-(all_by + 2) // 16) * 16
    right = wide_cols - all_by - 1
    cells = rows4 * wide_cols
    features = jnp.pad(features, ((0, 0), (1, right), (0, 0)))
    flags16 = jnp.pad(wide_flags.astype(jnp.bfloat16), ((0, 0), (1, right), (0, 0)))
    flat = jnp.pad(features.reshape(cells, FEAT), ((1, 1), (0, 0)))
    flat_flags = jnp.pad(flags16.reshape(cells, 9), ((1, 1), (0, 0)))
    span = own_bx * wide_cols
    pieces = []
    for row_step in range(3):
        for col_step in range(3):
            offset = row_step * 3 + col_step
            first = (2 - row_step) * wide_cols + (2 - col_step)
            pieces.append(
                flat[first : first + span] * flat_flags[first : first + span, offset : offset + 1]
            )
    stacked = jnp.concatenate(pieces, axis=-1)
    near_perm = jnp.dot(
        stacked, sur.reshape(9 * FEAT, OUTS), preferred_element_type=jnp.float32
    ).astype(jnp.bfloat16)
    own_rows = near_perm.reshape(own_bx, wide_cols, OUTS)
    table = jnp.pad(dft_table(total_cols), ((0, 0), (1, right), (0, 0)))
    norm_scale = 1.0 / math.sqrt(total_cols)
    lhs = own_rows.reshape(own_bx, wide_cols, 2, BS, NW * BS)
    parts = jnp.einsum("bYpji,jYq->bpiq", lhs, table, preferred_element_type=jnp.float32)
    real = parts[:, 0, :, :NK] + parts[:, 1, :, NK:]
    imag = parts[:, 1, :, :NK] - parts[:, 0, :, NK:]
    far_field = (jnp.stack([real, imag], axis=2) * norm_scale).reshape(own_bx * BS, NW, 2, NK)
    far_miss = (far_field - target_far.astype(jnp.float32)).astype(jnp.bfloat16)
    miss_above = lax.ppermute(far_miss[BS:], ("px", "py"), down)
    miss_below = lax.ppermute(far_miss[:BS], ("px", "py"), up)
    miss = jnp.concatenate([miss_above, far_miss, miss_below]).reshape(rows4, NW * BS, 2, NK)
    miss_re = miss[:, :, 0]
    miss_im = miss[:, :, 1]
    rhs = jnp.stack(
        [
            jnp.concatenate([miss_re, -miss_im], axis=-1),
            jnp.concatenate([miss_im, miss_re], axis=-1),
        ],
        axis=1,
    )
    adj_flat = jnp.einsum("bpiq,jYq->bYpji", rhs, table, preferred_element_type=jnp.float32)
    wide_adj = (adj_flat * norm_scale).astype(jnp.bfloat16).reshape(rows4, wide_cols, OUTS)
    feat_grad = jnp.zeros((own_bx, all_by, FEAT), jnp.float32)
    for row_step in range(3):
        for col_step in range(3):
            offset = row_step * 3 + col_step
            targets_at = wide_adj[row_step : row_step + own_bx, col_step : col_step + all_by]
            product = jnp.dot(
                targets_at.reshape(own_bx * all_by, OUTS),
                sur[offset].T,
                preferred_element_type=jnp.float32,
            )
            flags = own_flags[:, :, offset]
            feat_grad = feat_grad + flags[:, :, None] * product.reshape(own_bx, all_by, FEAT)
    unused, slopes = chebyshev_terms(width_blocks[1 : own_bx + 1], NF)
    grad_rows = feat_grad[:, :, : BS * BS] * slopes[0]
    for level in range(1, NF):
        grad_rows = grad_rows + feat_grad[:, :, level * BS * BS : (level + 1) * BS * BS] * slopes[level]
    near_grad = to_cells(grad_rows)
    framed = jnp.pad(wide_w[BS - 1 : BS + rows + 1], ((0, 0), (1, 1)))
    grad_tv = variation(framed, place * rows, 0, total_rows, total_cols)
    row_grad = near_grad + tv_weight * grad_tv
    width_grad = lax.all_to_all(row_grad, "py", 1, 0, tiled=True)
    return (far_field, width_grad)


def solution(mesh):
    return jax.shard_map(
        per_device,
        mesh=mesh,
        in_specs=(P("px", "py"), P("px", "py", None), P(), P(("px", "py"), None, None, None)),
        out_specs=(P(("px", "py"), None, None, None), P("px", "py")),
        check_vma=False,
    )
```

```python
import math

import jax
import jax.numpy as jnp
from jax import lax
from jax.sharding import PartitionSpec as P

BS = 8
NF = 4
NW = 8
NK = 512
FEAT = 256
OUTS = 1024


tv_weight = 0.5
tv_floor = 0.01


def with_halo(block, sides, width):
    for axis, dim in sides:
        count = lax.axis_size(axis)
        forward = [(i, i + 1) for i in range(count - 1)]
        backward = [(target, source) for source, target in forward]
        low = lax.ppermute(
            lax.slice_in_dim(block, block.shape[dim] - width, None, axis=dim), axis, forward
        )
        high = lax.ppermute(lax.slice_in_dim(block, 0, width, axis=dim), axis, backward)
        block = jnp.concatenate([low, block, high], axis=dim)
    return block


def chebyshev(normed, levels):
    values, slopes = ([], [])
    before = jnp.ones_like(normed)
    current = normed
    slope_before = jnp.zeros_like(normed)
    slope_now = jnp.ones_like(normed)
    for level in range(levels):
        values.append(current)
        slopes.append(slope_now)
        follow = 2.0 * normed * current - before
        slope_follow = 2.0 * current + 2.0 * normed * slope_now - slope_before
        before, current, slope_before, slope_now = (current, follow, slope_now, slope_follow)
    return (jnp.stack(values, 1), jnp.stack(slopes, 1))


def cell_blocks(planes, block_side):
    height, layers, columns = planes.shape
    shaped = planes.reshape(
        height // block_side, block_side, layers, columns // block_side, block_side
    )
    return shaped.transpose(0, 3, 1, 2, 4).reshape(
        height // block_side, columns // block_side, block_side * layers * block_side
    )


def block_cells(blocks, block_side, layers):
    block_rows, block_cols, unused = blocks.shape
    shaped = blocks.reshape(block_rows, block_cols, block_side, layers, block_side)
    return shaped.transpose(0, 2, 3, 1, 4).reshape(
        block_rows * block_side, layers, block_cols * block_side
    )


def field_rows(blocks, block_side, wave_count):
    block_rows, block_cols, unused = blocks.shape
    shaped = blocks.reshape(block_rows, block_cols, block_side, wave_count, 2 * block_side)
    return shaped.transpose(0, 2, 3, 1, 4).reshape(
        block_rows * block_side * wave_count, block_cols * 2 * block_side
    )


def rows_field(row_flat, block_side, wave_count):
    row_count, unused = row_flat.shape
    height = row_count // wave_count
    block_cols = unused // (2 * block_side)
    shaped = row_flat.reshape(
        height // block_side, block_side, wave_count, block_cols, 2 * block_side
    )
    return shaped.transpose(0, 3, 1, 2, 4).reshape(
        height // block_side, block_cols, block_side * wave_count * 2 * block_side
    )


def phase_table(first_col, col_count, total_cols):
    places = first_col + jnp.arange(col_count, dtype=jnp.int32)
    orders = jnp.arange(NK, dtype=jnp.int32) - NK // 2
    phase_turns = places[:, None] * orders[None, :] % total_cols
    angles = phase_turns.astype(jnp.float32) * (2.0 * math.pi / total_cols)
    cosine = jnp.cos(angles)
    sine_part = jnp.sin(angles)
    phase_rows = jnp.stack(
        [jnp.stack([cosine, -sine_part], 1), jnp.stack([sine_part, cosine], 1)], 1
    )
    phase_rows = phase_rows.astype(jnp.bfloat16).reshape(col_count // BS, BS, 2, 2 * NK)
    return phase_rows.transpose(0, 2, 1, 3).reshape(2 * col_count, 2 * NK)


def variation(framed, row_first, col_first, total_rows, total_cols):
    height = framed.shape[0] - 2
    columns = framed.shape[1] - 2
    step_down = framed[1:, :-1] - framed[:-1, :-1]
    step_right = framed[:-1, 1:] - framed[:-1, :-1]
    row_at = row_first - 1 + jnp.arange(height + 1, dtype=jnp.int32)
    col_at = col_first - 1 + jnp.arange(columns + 1, dtype=jnp.int32)
    step_down = jnp.where(((row_at >= 0) & (row_at < total_rows - 1))[:, None], step_down, 0.0)
    step_right = jnp.where(((col_at >= 0) & (col_at < total_cols - 1))[None, :], step_right, 0.0)
    magnitude = jnp.sqrt(step_down * step_down + step_right * step_right + tv_floor)
    flow_down = step_down / magnitude
    flow_right = step_right / magnitude
    return -(flow_down + flow_right)[1:, 1:] + flow_down[:-1, 1:] + flow_right[1:, :-1]


def lane_perm():
    rows = lax.broadcasted_iota(jnp.int32, (OUTS, OUTS), 0)
    cols = lax.broadcasted_iota(jnp.int32, (OUTS, OUTS), 1)
    inner = NW * BS
    hit = (rows // (2 * BS) == cols % inner) & (rows % (2 * BS) == cols // inner)
    return hit.astype(jnp.bfloat16)


def dft_table(total_cols):
    kk = jnp.arange(NK, dtype=jnp.int32) - NK // 2
    low = 8 * BS
    high = total_cols // low
    a = jnp.arange(high, dtype=jnp.int32)
    b = jnp.arange(low, dtype=jnp.int32)
    scale = 2.0 * math.pi / total_cols
    ta = ((a[:, None] * low * kk[None, :]) % total_cols).astype(jnp.float32) * scale
    tb = ((b[:, None] * kk[None, :]) % total_cols).astype(jnp.float32) * scale
    ca, sa = jnp.cos(ta), jnp.sin(ta)
    cb, sb = jnp.cos(tb), jnp.sin(tb)
    cb = cb.reshape(BS, BS, NK).transpose(1, 0, 2)
    sb = sb.reshape(BS, BS, NK).transpose(1, 0, 2)
    cos_v = ca[None, :, None, :] * cb[:, None, :, :] - sa[None, :, None, :] * sb[:, None, :, :]
    sin_v = sa[None, :, None, :] * cb[:, None, :, :] + ca[None, :, None, :] * sb[:, None, :, :]
    cos_v = cos_v.reshape(BS, total_cols // BS, NK)
    sin_v = sin_v.reshape(BS, total_cols // BS, NK)
    return jnp.concatenate([cos_v, sin_v], axis=-1).astype(jnp.bfloat16)


def to_blocks(cells):
    rows, cols = cells.shape
    shaped = cells.reshape(rows // BS, BS, cols // BS, BS).transpose(0, 2, 1, 3)
    return shaped.reshape(rows // BS, cols // BS, BS * BS)


def to_cells(blocks):
    rows, cols, unused = blocks.shape
    shaped = blocks.reshape(rows, cols, BS, BS).transpose(0, 2, 1, 3)
    return shaped.reshape(rows * BS, cols * BS)


def chebyshev_terms(normed, levels):
    values, slopes = ([], [])
    before = jnp.ones_like(normed)
    current = normed
    slope_before = jnp.zeros_like(normed)
    slope_now = jnp.ones_like(normed)
    for level in range(levels):
        values.append(current)
        slopes.append(slope_now)
        follow = 2.0 * normed * current - before
        slope_follow = 2.0 * current + 2.0 * normed * slope_now - slope_before
        before, current, slope_before, slope_now = (current, follow, slope_now, slope_follow)
    return values, slopes


def strip(cells, flags, total_cols, all_by):
    flag_rows = -(-all_by * 9 // total_cols)
    packed = jnp.pad(flags.reshape(-1), (0, flag_rows * total_cols - all_by * 9))
    return jnp.concatenate([cells, packed.reshape(flag_rows, total_cols)])


def unstrip(edge, all_by):
    return edge[:BS], edge[BS:].reshape(-1)[: all_by * 9].reshape(all_by, 9)


def per_device(widths, couplings, surrogate, target_far):
    height, columns = widths.shape
    groups = lax.axis_size("py")
    devices = lax.axis_size("px") * groups
    total_cols = columns * groups
    total_rows = height * lax.axis_size("px")
    rows = height // groups
    own_bx = rows // BS
    all_by = total_cols // BS
    block_cols = columns // BS
    place = lax.axis_index("px") * groups + lax.axis_index("py")
    down = [(i, i + 1) for i in range(devices - 1)]
    up = [(i + 1, i) for i in range(devices - 1)]
    block_rows = height // BS
    flag_vals = block_cols * 9
    flag_rows = -(-flag_vals // columns)
    packed_flags = jnp.pad(
        couplings.astype(jnp.float32).transpose(0, 2, 1).reshape(block_rows, flag_vals),
        ((0, 0), (0, flag_rows * columns - flag_vals)),
    ).reshape(block_rows, flag_rows, columns)
    count = lax.axis_size("px")
    forward = [(i, i + 1) for i in range(count - 1)]
    backward = [(i + 1, i) for i in range(count - 1)]
    low = lax.ppermute(
        jnp.concatenate([widths[height - BS :], packed_flags[block_rows - 1]]), "px", forward
    )
    high = lax.ppermute(jnp.concatenate([widths[:BS], packed_flags[0]]), "px", backward)
    tall_w = jnp.concatenate([low[:BS], widths, high[:BS]])
    tall_f = jnp.concatenate([low[BS:][None], packed_flags, high[BS:][None]])
    win_w = jnp.concatenate(
        [tall_w[:height].reshape(groups, rows, columns), tall_w[2 * BS :].reshape(groups, rows, columns)],
        axis=1,
    )
    win_f = jnp.concatenate(
        [
            tall_f[:block_rows].reshape(groups, own_bx * flag_rows, columns),
            tall_f[2:].reshape(groups, own_bx * flag_rows, columns),
        ],
        axis=1,
    )
    packed = jnp.concatenate([win_w, win_f], axis=1)
    packed, surrogate = lax.optimization_barrier((packed, surrogate))
    depth = packed.shape[1]
    got = lax.all_to_all(packed.reshape(groups * depth, columns), "py", 0, 1, tiled=True)
    rows4 = own_bx + 2
    wide_w = got[: 2 * rows]
    got_flags = got[2 * rows :].reshape(rows4, flag_rows, groups, columns).transpose(0, 2, 1, 3)
    got_flags = got_flags.reshape(rows4, groups, flag_rows * columns)[:, :, :flag_vals]
    wide_flags = got_flags.reshape(rows4, groups, 9, block_cols).transpose(0, 2, 1, 3)
    wide_flags = wide_flags.reshape(rows4, 9, all_by)
    own_flags = wide_flags[1 : own_bx + 1]
    width_blocks = lax.optimization_barrier(to_blocks(wide_w))
    values, unused = chebyshev_terms(width_blocks, NF)
    features = jnp.concatenate(values, axis=-1).astype(jnp.bfloat16)
    sur = surrogate.reshape(9, BS, NF, BS, OUTS).transpose(0, 2, 1, 3, 4).reshape(9, FEAT, OUTS)
    perm = lane_perm()
    sur = jnp.einsum("ofc,cd->ofd", sur, perm, preferred_element_type=jnp.float32).astype(
        jnp.bfloat16
    )
    wide_cols = -(-(all_by + 2) // 16) * 16
    right = wide_cols - all_by - 1
    cells = rows4 * wide_cols
    features = jnp.pad(features, ((0, 0), (1, right), (0, 0)))
    flags16 = jnp.pad(wide_flags.astype(jnp.bfloat16), ((0, 0), (0, 0), (1, right)))
    flat = jnp.pad(features.reshape(cells, FEAT), ((1, 1), (0, 0)))
    flat_flags = jnp.pad(flags16.transpose(1, 0, 2).reshape(9, cells), ((0, 0), (1, 1)))
    span = own_bx * wide_cols
    pieces = []
    for row_step in range(3):
        for col_step in range(3):
            offset = row_step * 3 + col_step
            first = (2 - row_step) * wide_cols + (2 - col_step)
            pieces.append(
                flat[first : first + span] * flat_flags[offset, first : first + span][:, None]
            )
    stacked = jnp.concatenate(pieces, axis=-1)
    near_perm = jnp.dot(
        stacked, sur.reshape(9 * FEAT, OUTS), preferred_element_type=jnp.float32
    ).astype(jnp.bfloat16)
    own_rows = near_perm.reshape(own_bx, wide_cols, OUTS)
    table = jnp.pad(dft_table(total_cols), ((0, 0), (1, right), (0, 0)))
    norm_scale = 1.0 / math.sqrt(total_cols)
    lhs = own_rows.reshape(own_bx, wide_cols, 2, BS, NW * BS)
    parts = jnp.einsum("bYpji,jYq->bpiq", lhs, table, preferred_element_type=jnp.float32)
    real = parts[:, 0, :, :NK] + parts[:, 1, :, NK:]
    imag = parts[:, 1, :, :NK] - parts[:, 0, :, NK:]
    far_field = (jnp.stack([real, imag], axis=2) * norm_scale).reshape(own_bx * BS, NW, 2, NK)
    far_miss = (far_field - target_far.astype(jnp.float32)).astype(jnp.bfloat16)
    miss_above = lax.ppermute(far_miss[BS:], ("px", "py"), down)
    miss_below = lax.ppermute(far_miss[:BS], ("px", "py"), up)
    miss = jnp.concatenate([miss_above, far_miss, miss_below]).reshape(rows4, NW * BS, 2, NK)
    miss_re = miss[:, :, 0]
    miss_im = miss[:, :, 1]
    rhs = jnp.stack(
        [
            jnp.concatenate([miss_re, -miss_im], axis=-1),
            jnp.concatenate([miss_im, miss_re], axis=-1),
        ],
        axis=1,
    )
    adj_flat = jnp.einsum("bpiq,jYq->bYpji", rhs, table, preferred_element_type=jnp.float32)
    wide_adj = (adj_flat * norm_scale).astype(jnp.bfloat16).reshape(rows4, wide_cols, OUTS)
    feat_grad = jnp.zeros((own_bx, all_by, FEAT), jnp.float32)
    for row_step in range(3):
        for col_step in range(3):
            offset = row_step * 3 + col_step
            targets_at = wide_adj[row_step : row_step + own_bx, col_step : col_step + all_by]
            product = jnp.dot(
                targets_at.reshape(own_bx * all_by, OUTS),
                sur[offset].T,
                preferred_element_type=jnp.float32,
            )
            flags = own_flags[:, offset, :]
            feat_grad = feat_grad + flags[:, :, None] * product.reshape(own_bx, all_by, FEAT)
    unused, slopes = chebyshev_terms(width_blocks[1 : own_bx + 1], NF)
    grad_rows = feat_grad[:, :, : BS * BS] * slopes[0]
    for level in range(1, NF):
        grad_rows = grad_rows + feat_grad[:, :, level * BS * BS : (level + 1) * BS * BS] * slopes[level]
    near_grad = to_cells(grad_rows)
    framed = jnp.pad(wide_w[BS - 1 : BS + rows + 1], ((0, 0), (1, 1)))
    grad_tv = variation(framed, place * rows, 0, total_rows, total_cols)
    row_grad = near_grad + tv_weight * grad_tv
    width_grad = lax.all_to_all(row_grad, "py", 1, 0, tiled=True)
    return (far_field, width_grad)


def solution(mesh):
    return jax.shard_map(
        per_device,
        mesh=mesh,
        in_specs=(P("px", "py"), P("px", "py", None), P(), P(("px", "py"), None, None, None)),
        out_specs=(P(("px", "py"), None, None, None), P("px", "py")),
        check_vma=False,
    )
```

```python
import math

import jax
import jax.numpy as jnp
from jax import lax
from jax.sharding import PartitionSpec as P

BS = 8
NF = 4
NW = 8
NK = 512
FEAT = 256
OUTS = 1024


tv_weight = 0.5
tv_floor = 0.01


def with_halo(block, sides, width):
    for axis, dim in sides:
        count = lax.axis_size(axis)
        forward = [(i, i + 1) for i in range(count - 1)]
        backward = [(target, source) for source, target in forward]
        low = lax.ppermute(
            lax.slice_in_dim(block, block.shape[dim] - width, None, axis=dim), axis, forward
        )
        high = lax.ppermute(lax.slice_in_dim(block, 0, width, axis=dim), axis, backward)
        block = jnp.concatenate([low, block, high], axis=dim)
    return block


def chebyshev(normed, levels):
    values, slopes = ([], [])
    before = jnp.ones_like(normed)
    current = normed
    slope_before = jnp.zeros_like(normed)
    slope_now = jnp.ones_like(normed)
    for level in range(levels):
        values.append(current)
        slopes.append(slope_now)
        follow = 2.0 * normed * current - before
        slope_follow = 2.0 * current + 2.0 * normed * slope_now - slope_before
        before, current, slope_before, slope_now = (current, follow, slope_now, slope_follow)
    return (jnp.stack(values, 1), jnp.stack(slopes, 1))


def cell_blocks(planes, block_side):
    height, layers, columns = planes.shape
    shaped = planes.reshape(
        height // block_side, block_side, layers, columns // block_side, block_side
    )
    return shaped.transpose(0, 3, 1, 2, 4).reshape(
        height // block_side, columns // block_side, block_side * layers * block_side
    )


def block_cells(blocks, block_side, layers):
    block_rows, block_cols, unused = blocks.shape
    shaped = blocks.reshape(block_rows, block_cols, block_side, layers, block_side)
    return shaped.transpose(0, 2, 3, 1, 4).reshape(
        block_rows * block_side, layers, block_cols * block_side
    )


def field_rows(blocks, block_side, wave_count):
    block_rows, block_cols, unused = blocks.shape
    shaped = blocks.reshape(block_rows, block_cols, block_side, wave_count, 2 * block_side)
    return shaped.transpose(0, 2, 3, 1, 4).reshape(
        block_rows * block_side * wave_count, block_cols * 2 * block_side
    )


def rows_field(row_flat, block_side, wave_count):
    row_count, unused = row_flat.shape
    height = row_count // wave_count
    block_cols = unused // (2 * block_side)
    shaped = row_flat.reshape(
        height // block_side, block_side, wave_count, block_cols, 2 * block_side
    )
    return shaped.transpose(0, 3, 1, 2, 4).reshape(
        height // block_side, block_cols, block_side * wave_count * 2 * block_side
    )


def phase_table(first_col, col_count, total_cols):
    places = first_col + jnp.arange(col_count, dtype=jnp.int32)
    orders = jnp.arange(NK, dtype=jnp.int32) - NK // 2
    phase_turns = places[:, None] * orders[None, :] % total_cols
    angles = phase_turns.astype(jnp.float32) * (2.0 * math.pi / total_cols)
    cosine = jnp.cos(angles)
    sine_part = jnp.sin(angles)
    phase_rows = jnp.stack(
        [jnp.stack([cosine, -sine_part], 1), jnp.stack([sine_part, cosine], 1)], 1
    )
    phase_rows = phase_rows.astype(jnp.bfloat16).reshape(col_count // BS, BS, 2, 2 * NK)
    return phase_rows.transpose(0, 2, 1, 3).reshape(2 * col_count, 2 * NK)


def variation(framed, row_first, col_first, total_rows, total_cols):
    height = framed.shape[0] - 2
    columns = framed.shape[1] - 2
    step_down = framed[1:, :-1] - framed[:-1, :-1]
    step_right = framed[:-1, 1:] - framed[:-1, :-1]
    row_at = row_first - 1 + jnp.arange(height + 1, dtype=jnp.int32)
    col_at = col_first - 1 + jnp.arange(columns + 1, dtype=jnp.int32)
    step_down = jnp.where(((row_at >= 0) & (row_at < total_rows - 1))[:, None], step_down, 0.0)
    step_right = jnp.where(((col_at >= 0) & (col_at < total_cols - 1))[None, :], step_right, 0.0)
    magnitude = jnp.sqrt(step_down * step_down + step_right * step_right + tv_floor)
    flow_down = step_down / magnitude
    flow_right = step_right / magnitude
    return -(flow_down + flow_right)[1:, 1:] + flow_down[:-1, 1:] + flow_right[1:, :-1]


def lane_perm():
    rows = lax.broadcasted_iota(jnp.int32, (OUTS, OUTS), 0)
    cols = lax.broadcasted_iota(jnp.int32, (OUTS, OUTS), 1)
    inner = NW * BS
    same_iw = rows // (2 * BS) == cols % inner
    same_p = (rows // BS) % 2 == (cols // inner) % 2
    same_j = rows % BS == cols // (2 * inner)
    hit = same_iw & same_p & same_j
    return hit.astype(jnp.bfloat16)


def dft_table(total_cols):
    kk = jnp.arange(NK, dtype=jnp.int32) - NK // 2
    low = 8 * BS
    high = total_cols // low
    a = jnp.arange(high, dtype=jnp.int32)
    b = jnp.arange(low, dtype=jnp.int32)
    scale = 2.0 * math.pi / total_cols
    ta = ((a[:, None] * low * kk[None, :]) % total_cols).astype(jnp.float32) * scale
    tb = ((b[:, None] * kk[None, :]) % total_cols).astype(jnp.float32) * scale
    ca, sa = jnp.cos(ta), jnp.sin(ta)
    cb, sb = jnp.cos(tb), jnp.sin(tb)
    cb = cb.reshape(BS, BS, NK)
    sb = sb.reshape(BS, BS, NK)
    cos_v = ca[:, None, None, :] * cb[None] - sa[:, None, None, :] * sb[None]
    sin_v = sa[:, None, None, :] * cb[None] + ca[:, None, None, :] * sb[None]
    cos_v = cos_v.reshape(total_cols // BS, BS, NK)
    sin_v = sin_v.reshape(total_cols // BS, BS, NK)
    return jnp.concatenate([cos_v, sin_v], axis=-1).astype(jnp.bfloat16)


def to_blocks(cells):
    rows, cols = cells.shape
    shaped = cells.reshape(rows // BS, BS, cols // BS, BS).transpose(0, 2, 1, 3)
    return shaped.reshape(rows // BS, cols // BS, BS * BS)


def to_cells(blocks):
    rows, cols, unused = blocks.shape
    shaped = blocks.reshape(rows, cols, BS, BS).transpose(0, 2, 1, 3)
    return shaped.reshape(rows * BS, cols * BS)


def chebyshev_terms(normed, levels):
    values, slopes = ([], [])
    before = jnp.ones_like(normed)
    current = normed
    slope_before = jnp.zeros_like(normed)
    slope_now = jnp.ones_like(normed)
    for level in range(levels):
        values.append(current)
        slopes.append(slope_now)
        follow = 2.0 * normed * current - before
        slope_follow = 2.0 * current + 2.0 * normed * slope_now - slope_before
        before, current, slope_before, slope_now = (current, follow, slope_now, slope_follow)
    return values, slopes


def strip(cells, flags, total_cols, all_by):
    flag_rows = -(-all_by * 9 // total_cols)
    packed = jnp.pad(flags.reshape(-1), (0, flag_rows * total_cols - all_by * 9))
    return jnp.concatenate([cells, packed.reshape(flag_rows, total_cols)])


def unstrip(edge, all_by):
    return edge[:BS], edge[BS:].reshape(-1)[: all_by * 9].reshape(all_by, 9)


def per_device(widths, couplings, surrogate, target_far):
    height, columns = widths.shape
    groups = lax.axis_size("py")
    devices = lax.axis_size("px") * groups
    total_cols = columns * groups
    total_rows = height * lax.axis_size("px")
    rows = height // groups
    own_bx = rows // BS
    all_by = total_cols // BS
    block_cols = columns // BS
    place = lax.axis_index("px") * groups + lax.axis_index("py")
    down = [(i, i + 1) for i in range(devices - 1)]
    up = [(i + 1, i) for i in range(devices - 1)]
    block_rows = height // BS
    flag_vals = block_cols * 9
    flag_rows = -(-flag_vals // columns)
    packed_flags = jnp.pad(
        couplings.astype(jnp.float32).reshape(block_rows, flag_vals),
        ((0, 0), (0, flag_rows * columns - flag_vals)),
    ).reshape(block_rows, flag_rows, columns)
    count = lax.axis_size("px")
    forward = [(i, i + 1) for i in range(count - 1)]
    backward = [(i + 1, i) for i in range(count - 1)]
    low = lax.ppermute(
        jnp.concatenate([widths[height - BS :], packed_flags[block_rows - 1]]), "px", forward
    )
    high = lax.ppermute(jnp.concatenate([widths[:BS], packed_flags[0]]), "px", backward)
    tall_w = jnp.concatenate([low[:BS], widths, high[:BS]])
    tall_f = jnp.concatenate([low[BS:][None], packed_flags, high[BS:][None]])
    win_w = jnp.concatenate(
        [tall_w[:height].reshape(groups, rows, columns), tall_w[2 * BS :].reshape(groups, rows, columns)],
        axis=1,
    )
    win_f = jnp.concatenate(
        [
            tall_f[:block_rows].reshape(groups, own_bx * flag_rows, columns),
            tall_f[2:].reshape(groups, own_bx * flag_rows, columns),
        ],
        axis=1,
    )
    packed = jnp.concatenate([win_w, win_f], axis=1)
    packed, surrogate = lax.optimization_barrier((packed, surrogate))
    depth = packed.shape[1]
    got = lax.all_to_all(packed.reshape(groups * depth, columns), "py", 0, 1, tiled=True)
    rows4 = own_bx + 2
    wide_w = got[: 2 * rows]
    got_flags = got[2 * rows :].reshape(rows4, flag_rows, groups, columns).transpose(0, 2, 1, 3)
    got_flags = got_flags.reshape(rows4, groups, flag_rows * columns)[:, :, :flag_vals]
    wide_flags = got_flags.reshape(rows4, all_by, 9)
    own_flags = wide_flags[1 : own_bx + 1]
    width_blocks = lax.optimization_barrier(to_blocks(wide_w))
    values, unused = chebyshev_terms(width_blocks, NF)
    features = jnp.concatenate(values, axis=-1).astype(jnp.bfloat16)
    sur = surrogate.reshape(9, BS, NF, BS, OUTS).transpose(0, 2, 1, 3, 4).reshape(9, FEAT, OUTS)
    perm = lane_perm()
    sur = jnp.einsum("ofc,cd->ofd", sur, perm, preferred_element_type=jnp.float32).astype(
        jnp.bfloat16
    )
    wide_cols = -(-(all_by + 2) // 16) * 16
    right = wide_cols - all_by - 1
    cells = rows4 * wide_cols
    features = jnp.pad(features, ((0, 0), (1, right), (0, 0)))
    flags16 = jnp.pad(wide_flags.astype(jnp.bfloat16), ((0, 0), (1, right), (0, 0)))
    flat = jnp.pad(features.reshape(cells, FEAT), ((1, 1), (0, 0)))
    flat_flags = jnp.pad(flags16.reshape(cells, 9), ((1, 1), (0, 0)))
    span = own_bx * wide_cols
    pieces = []
    for row_step in range(3):
        for col_step in range(3):
            offset = row_step * 3 + col_step
            first = (2 - row_step) * wide_cols + (2 - col_step)
            pieces.append(
                flat[first : first + span] * flat_flags[first : first + span, offset : offset + 1]
            )
    stacked = jnp.concatenate(pieces, axis=-1)
    near_perm = jnp.dot(
        stacked, sur.reshape(9 * FEAT, OUTS), preferred_element_type=jnp.float32
    ).astype(jnp.bfloat16)
    own_rows = near_perm.reshape(own_bx, wide_cols, OUTS)
    table = jnp.pad(dft_table(total_cols), ((1, right), (0, 0), (0, 0)))
    norm_scale = 1.0 / math.sqrt(total_cols)
    lhs = own_rows.reshape(own_bx, wide_cols, BS, 2 * NW * BS)
    parts = jnp.einsum("bYjc,Yjq->bcq", lhs, table, preferred_element_type=jnp.float32)
    parts = parts.reshape(own_bx, 2, NW * BS, 2 * NK)
    real = parts[:, 0, :, :NK] + parts[:, 1, :, NK:]
    imag = parts[:, 1, :, :NK] - parts[:, 0, :, NK:]
    far_field = (jnp.stack([real, imag], axis=2) * norm_scale).reshape(own_bx * BS, NW, 2, NK)
    far_miss = (far_field - target_far.astype(jnp.float32)).astype(jnp.bfloat16)
    miss_above = lax.ppermute(far_miss[BS:], ("px", "py"), down)
    miss_below = lax.ppermute(far_miss[:BS], ("px", "py"), up)
    miss = jnp.concatenate([miss_above, far_miss, miss_below]).reshape(rows4, NW * BS, 2, NK)
    miss_re = miss[:, :, 0]
    miss_im = miss[:, :, 1]
    rhs = jnp.stack(
        [
            jnp.concatenate([miss_re, -miss_im], axis=-1),
            jnp.concatenate([miss_im, miss_re], axis=-1),
        ],
        axis=1,
    )
    rhs = rhs.reshape(rows4, 2 * NW * BS, 2 * NK)
    adj_flat = jnp.einsum("bcq,Yjq->bYjc", rhs, table, preferred_element_type=jnp.float32)
    wide_adj = (adj_flat * norm_scale).astype(jnp.bfloat16).reshape(rows4, wide_cols, OUTS)
    feat_grad = jnp.zeros((own_bx, all_by, FEAT), jnp.float32)
    for row_step in range(3):
        for col_step in range(3):
            offset = row_step * 3 + col_step
            targets_at = wide_adj[row_step : row_step + own_bx, col_step : col_step + all_by]
            product = jnp.dot(
                targets_at.reshape(own_bx * all_by, OUTS),
                sur[offset].T,
                preferred_element_type=jnp.float32,
            )
            flags = own_flags[:, :, offset]
            feat_grad = feat_grad + flags[:, :, None] * product.reshape(own_bx, all_by, FEAT)
    unused, slopes = chebyshev_terms(width_blocks[1 : own_bx + 1], NF)
    grad_rows = feat_grad[:, :, : BS * BS] * slopes[0]
    for level in range(1, NF):
        grad_rows = grad_rows + feat_grad[:, :, level * BS * BS : (level + 1) * BS * BS] * slopes[level]
    near_grad = to_cells(grad_rows)
    framed = jnp.pad(wide_w[BS - 1 : BS + rows + 1], ((0, 0), (1, 1)))
    grad_tv = variation(framed, place * rows, 0, total_rows, total_cols)
    row_grad = near_grad + tv_weight * grad_tv
    width_grad = lax.all_to_all(row_grad, "py", 1, 0, tiled=True)
    return (far_field, width_grad)


def solution(mesh):
    return jax.shard_map(
        per_device,
        mesh=mesh,
        in_specs=(P("px", "py"), P("px", "py", None), P(), P(("px", "py"), None, None, None)),
        out_specs=(P(("px", "py"), None, None, None), P("px", "py")),
        check_vma=False,
    )
```

```python
import math

import jax
import jax.numpy as jnp
from jax import lax
from jax.sharding import PartitionSpec as P

BS = 8
NF = 4
NW = 8
NK = 512
FEAT = 256
OUTS = 1024


tv_weight = 0.5
tv_floor = 0.01


def with_halo(block, sides, width):
    for axis, dim in sides:
        count = lax.axis_size(axis)
        forward = [(i, i + 1) for i in range(count - 1)]
        backward = [(target, source) for source, target in forward]
        low = lax.ppermute(
            lax.slice_in_dim(block, block.shape[dim] - width, None, axis=dim), axis, forward
        )
        high = lax.ppermute(lax.slice_in_dim(block, 0, width, axis=dim), axis, backward)
        block = jnp.concatenate([low, block, high], axis=dim)
    return block


def chebyshev(normed, levels):
    values, slopes = ([], [])
    before = jnp.ones_like(normed)
    current = normed
    slope_before = jnp.zeros_like(normed)
    slope_now = jnp.ones_like(normed)
    for level in range(levels):
        values.append(current)
        slopes.append(slope_now)
        follow = 2.0 * normed * current - before
        slope_follow = 2.0 * current + 2.0 * normed * slope_now - slope_before
        before, current, slope_before, slope_now = (current, follow, slope_now, slope_follow)
    return (jnp.stack(values, 1), jnp.stack(slopes, 1))


def cell_blocks(planes, block_side):
    height, layers, columns = planes.shape
    shaped = planes.reshape(
        height // block_side, block_side, layers, columns // block_side, block_side
    )
    return shaped.transpose(0, 3, 1, 2, 4).reshape(
        height // block_side, columns // block_side, block_side * layers * block_side
    )


def block_cells(blocks, block_side, layers):
    block_rows, block_cols, unused = blocks.shape
    shaped = blocks.reshape(block_rows, block_cols, block_side, layers, block_side)
    return shaped.transpose(0, 2, 3, 1, 4).reshape(
        block_rows * block_side, layers, block_cols * block_side
    )


def field_rows(blocks, block_side, wave_count):
    block_rows, block_cols, unused = blocks.shape
    shaped = blocks.reshape(block_rows, block_cols, block_side, wave_count, 2 * block_side)
    return shaped.transpose(0, 2, 3, 1, 4).reshape(
        block_rows * block_side * wave_count, block_cols * 2 * block_side
    )


def rows_field(row_flat, block_side, wave_count):
    row_count, unused = row_flat.shape
    height = row_count // wave_count
    block_cols = unused // (2 * block_side)
    shaped = row_flat.reshape(
        height // block_side, block_side, wave_count, block_cols, 2 * block_side
    )
    return shaped.transpose(0, 3, 1, 2, 4).reshape(
        height // block_side, block_cols, block_side * wave_count * 2 * block_side
    )


def phase_table(first_col, col_count, total_cols):
    places = first_col + jnp.arange(col_count, dtype=jnp.int32)
    orders = jnp.arange(NK, dtype=jnp.int32) - NK // 2
    phase_turns = places[:, None] * orders[None, :] % total_cols
    angles = phase_turns.astype(jnp.float32) * (2.0 * math.pi / total_cols)
    cosine = jnp.cos(angles)
    sine_part = jnp.sin(angles)
    phase_rows = jnp.stack(
        [jnp.stack([cosine, -sine_part], 1), jnp.stack([sine_part, cosine], 1)], 1
    )
    phase_rows = phase_rows.astype(jnp.bfloat16).reshape(col_count // BS, BS, 2, 2 * NK)
    return phase_rows.transpose(0, 2, 1, 3).reshape(2 * col_count, 2 * NK)


def variation(framed, row_first, col_first, total_rows, total_cols):
    height = framed.shape[0] - 2
    columns = framed.shape[1] - 2
    step_down = framed[1:, :-1] - framed[:-1, :-1]
    step_right = framed[:-1, 1:] - framed[:-1, :-1]
    row_at = row_first - 1 + jnp.arange(height + 1, dtype=jnp.int32)
    col_at = col_first - 1 + jnp.arange(columns + 1, dtype=jnp.int32)
    step_down = jnp.where(((row_at >= 0) & (row_at < total_rows - 1))[:, None], step_down, 0.0)
    step_right = jnp.where(((col_at >= 0) & (col_at < total_cols - 1))[None, :], step_right, 0.0)
    magnitude = jnp.sqrt(step_down * step_down + step_right * step_right + tv_floor)
    flow_down = step_down / magnitude
    flow_right = step_right / magnitude
    return -(flow_down + flow_right)[1:, 1:] + flow_down[:-1, 1:] + flow_right[1:, :-1]


def lane_perm():
    rows = lax.broadcasted_iota(jnp.int32, (OUTS, OUTS), 0)
    cols = lax.broadcasted_iota(jnp.int32, (OUTS, OUTS), 1)
    inner = NW * BS
    hit = (rows // (2 * BS) == cols % inner) & (rows % (2 * BS) == cols // inner)
    return hit.astype(jnp.bfloat16)


def dft_table(total_cols):
    kk = jnp.arange(NK, dtype=jnp.int32) - NK // 2
    low = 8 * BS
    high = total_cols // low
    a = jnp.arange(high, dtype=jnp.int32)
    b = jnp.arange(low, dtype=jnp.int32)
    scale = 2.0 * math.pi / total_cols
    ta = ((a[:, None] * low * kk[None, :]) % total_cols).astype(jnp.float32) * scale
    tb = ((b[:, None] * kk[None, :]) % total_cols).astype(jnp.float32) * scale
    ca, sa = jnp.cos(ta), jnp.sin(ta)
    cb, sb = jnp.cos(tb), jnp.sin(tb)
    cb = cb.reshape(BS, BS, NK).transpose(1, 0, 2)
    sb = sb.reshape(BS, BS, NK).transpose(1, 0, 2)
    cos_v = ca[None, :, None, :] * cb[:, None, :, :] - sa[None, :, None, :] * sb[:, None, :, :]
    sin_v = sa[None, :, None, :] * cb[:, None, :, :] + ca[None, :, None, :] * sb[:, None, :, :]
    cos_v = cos_v.reshape(BS, total_cols // BS, NK)
    sin_v = sin_v.reshape(BS, total_cols // BS, NK)
    return jnp.concatenate([cos_v, sin_v], axis=-1).astype(jnp.bfloat16)


def to_blocks(cells):
    rows, cols = cells.shape
    shaped = cells.reshape(rows // BS, BS, cols // BS, BS).transpose(0, 2, 1, 3)
    return shaped.reshape(rows // BS, cols // BS, BS * BS)


def to_cells(blocks):
    rows, cols, unused = blocks.shape
    shaped = blocks.reshape(rows, cols, BS, BS).transpose(0, 2, 1, 3)
    return shaped.reshape(rows * BS, cols * BS)


def chebyshev_terms(normed, levels):
    values, slopes = ([], [])
    before = jnp.ones_like(normed)
    current = normed
    slope_before = jnp.zeros_like(normed)
    slope_now = jnp.ones_like(normed)
    for level in range(levels):
        values.append(current)
        slopes.append(slope_now)
        follow = 2.0 * normed * current - before
        slope_follow = 2.0 * current + 2.0 * normed * slope_now - slope_before
        before, current, slope_before, slope_now = (current, follow, slope_now, slope_follow)
    return values, slopes


def strip(cells, flags, total_cols, all_by):
    flag_rows = -(-all_by * 9 // total_cols)
    packed = jnp.pad(flags.reshape(-1), (0, flag_rows * total_cols - all_by * 9))
    return jnp.concatenate([cells, packed.reshape(flag_rows, total_cols)])


def unstrip(edge, all_by):
    return edge[:BS], edge[BS:].reshape(-1)[: all_by * 9].reshape(all_by, 9)


def per_device(widths, couplings, surrogate, target_far):
    height, columns = widths.shape
    groups = lax.axis_size("py")
    devices = lax.axis_size("px") * groups
    total_cols = columns * groups
    total_rows = height * lax.axis_size("px")
    rows = height // groups
    own_bx = rows // BS
    all_by = total_cols // BS
    block_cols = columns // BS
    place = lax.axis_index("px") * groups + lax.axis_index("py")
    down = [(i, i + 1) for i in range(devices - 1)]
    up = [(i + 1, i) for i in range(devices - 1)]
    block_rows = height // BS
    flag_vals = block_cols * 9
    flag_rows = -(-flag_vals // columns)
    packed_flags = jnp.pad(
        couplings.astype(jnp.float32).reshape(block_rows, flag_vals),
        ((0, 0), (0, flag_rows * columns - flag_vals)),
    ).reshape(block_rows, flag_rows, columns)
    count = lax.axis_size("px")
    forward = [(i, i + 1) for i in range(count - 1)]
    backward = [(i + 1, i) for i in range(count - 1)]
    low = lax.ppermute(
        jnp.concatenate([widths[height - BS :], packed_flags[block_rows - 1]]), "px", forward
    )
    high = lax.ppermute(jnp.concatenate([widths[:BS], packed_flags[0]]), "px", backward)
    tall_w = jnp.concatenate([low[:BS], widths, high[:BS]])
    tall_f = jnp.concatenate([low[BS:][None], packed_flags, high[BS:][None]])
    win_w = jnp.concatenate(
        [tall_w[:height].reshape(groups, rows, columns), tall_w[2 * BS :].reshape(groups, rows, columns)],
        axis=1,
    )
    win_f = jnp.concatenate(
        [
            tall_f[:block_rows].reshape(groups, own_bx * flag_rows, columns),
            tall_f[2:].reshape(groups, own_bx * flag_rows, columns),
        ],
        axis=1,
    )
    packed = jnp.concatenate([win_w, win_f], axis=1)
    packed, surrogate = lax.optimization_barrier((packed, surrogate))
    depth = packed.shape[1]
    got = lax.all_to_all(packed.reshape(groups * depth, columns), "py", 0, 1, tiled=True)
    rows4 = own_bx + 2
    wide_w = got[: 2 * rows]
    got_flags = got[2 * rows :].reshape(rows4, flag_rows, groups, columns).transpose(0, 2, 1, 3)
    got_flags = got_flags.reshape(rows4, groups, flag_rows * columns)[:, :, :flag_vals]
    wide_flags = got_flags.reshape(rows4, all_by, 9)
    own_flags = wide_flags[1 : own_bx + 1]
    width_blocks = lax.optimization_barrier(to_blocks(wide_w))
    values, unused = chebyshev_terms(width_blocks, NF)
    features = jnp.concatenate(values, axis=-1).astype(jnp.bfloat16)
    sur = surrogate.reshape(9, BS, NF, BS, OUTS).transpose(0, 2, 1, 3, 4).reshape(9, FEAT, OUTS)
    perm = lane_perm()
    sur = jnp.einsum("ofc,cd->ofd", sur, perm, preferred_element_type=jnp.float32).astype(
        jnp.bfloat16
    )
    wide_cols = -(-(all_by + 2) // 16) * 16
    right = wide_cols - all_by - 1
    cells = rows4 * wide_cols
    features = jnp.pad(features, ((0, 0), (1, right), (0, 0)))
    flags16 = jnp.pad(wide_flags.astype(jnp.bfloat16), ((0, 0), (1, right), (0, 0)))
    flat = jnp.pad(features.reshape(cells, FEAT), ((1, 1), (0, 0)))
    flat_flags = jnp.pad(flags16.reshape(cells, 9), ((1, 1), (0, 0)))
    span = own_bx * wide_cols
    pieces = []
    for row_step in range(3):
        for col_step in range(3):
            offset = row_step * 3 + col_step
            first = (2 - row_step) * wide_cols + (2 - col_step)
            pieces.append(
                flat[first : first + span] * flat_flags[first : first + span, offset : offset + 1]
            )
    stacked = jnp.concatenate(pieces, axis=-1)
    near_perm = jnp.dot(
        stacked, sur.reshape(9 * FEAT, OUTS), preferred_element_type=jnp.float32
    ).astype(jnp.bfloat16)
    own_rows = near_perm.reshape(own_bx, wide_cols, OUTS)
    table = jnp.pad(dft_table(total_cols), ((0, 0), (1, right), (0, 0)))
    norm_scale = 1.0 / math.sqrt(total_cols)
    lhs = own_rows.reshape(own_bx, wide_cols, 2, BS, NW * BS)
    parts = jnp.einsum("bYpji,jYq->bpiq", lhs, table, preferred_element_type=jnp.float32)
    real = parts[:, 0, :, :NK] + parts[:, 1, :, NK:]
    imag = parts[:, 1, :, :NK] - parts[:, 0, :, NK:]
    far_field = (jnp.stack([real, imag], axis=2) * norm_scale).reshape(own_bx * BS, NW, 2, NK)
    far_miss = (far_field - target_far.astype(jnp.float32)).astype(jnp.bfloat16)
    miss_above = lax.ppermute(far_miss[BS:], ("px", "py"), down)
    miss_below = lax.ppermute(far_miss[:BS], ("px", "py"), up)
    def adjoint(miss_rows):
        miss_rows = miss_rows.reshape(-1, NW * BS, 2, NK)
        miss_re = miss_rows[:, :, 0]
        miss_im = miss_rows[:, :, 1]
        rhs = jnp.stack(
            [
                jnp.concatenate([miss_re, -miss_im], axis=-1),
                jnp.concatenate([miss_im, miss_re], axis=-1),
            ],
            axis=1,
        )
        adj_flat = jnp.einsum("bpiq,jYq->bYpji", rhs, table, preferred_element_type=jnp.float32)
        return (adj_flat * norm_scale).astype(jnp.bfloat16).reshape(-1, wide_cols, OUTS)

    adj_own = adjoint(far_miss)
    adj_near = adjoint(jnp.concatenate([miss_above, miss_below]))
    wide_adj = jnp.concatenate([adj_near[:1], adj_own, adj_near[1:]])
    feat_grad = jnp.zeros((own_bx, all_by, FEAT), jnp.float32)
    for row_step in range(3):
        for col_step in range(3):
            offset = row_step * 3 + col_step
            targets_at = wide_adj[row_step : row_step + own_bx, col_step : col_step + all_by]
            product = jnp.dot(
                targets_at.reshape(own_bx * all_by, OUTS),
                sur[offset].T,
                preferred_element_type=jnp.float32,
            )
            flags = own_flags[:, :, offset]
            feat_grad = feat_grad + flags[:, :, None] * product.reshape(own_bx, all_by, FEAT)
    unused, slopes = chebyshev_terms(width_blocks[1 : own_bx + 1], NF)
    grad_rows = feat_grad[:, :, : BS * BS] * slopes[0]
    for level in range(1, NF):
        grad_rows = grad_rows + feat_grad[:, :, level * BS * BS : (level + 1) * BS * BS] * slopes[level]
    near_grad = to_cells(grad_rows)
    framed = jnp.pad(wide_w[BS - 1 : BS + rows + 1], ((0, 0), (1, 1)))
    grad_tv = variation(framed, place * rows, 0, total_rows, total_cols)
    row_grad = near_grad + tv_weight * grad_tv
    width_grad = lax.all_to_all(row_grad, "py", 1, 0, tiled=True)
    return (far_field, width_grad)


def solution(mesh):
    return jax.shard_map(
        per_device,
        mesh=mesh,
        in_specs=(P("px", "py"), P("px", "py", None), P(), P(("px", "py"), None, None, None)),
        out_specs=(P(("px", "py"), None, None, None), P("px", "py")),
        check_vma=False,
    )
```

```python
import math

import jax
import jax.numpy as jnp
from jax import lax
from jax.sharding import PartitionSpec as P

BS = 8
NF = 4
NW = 8
NK = 512
FEAT = 256
OUTS = 1024


tv_weight = 0.5
tv_floor = 0.01


def with_halo(block, sides, width):
    for axis, dim in sides:
        count = lax.axis_size(axis)
        forward = [(i, i + 1) for i in range(count - 1)]
        backward = [(target, source) for source, target in forward]
        low = lax.ppermute(
            lax.slice_in_dim(block, block.shape[dim] - width, None, axis=dim), axis, forward
        )
        high = lax.ppermute(lax.slice_in_dim(block, 0, width, axis=dim), axis, backward)
        block = jnp.concatenate([low, block, high], axis=dim)
    return block


def chebyshev(normed, levels):
    values, slopes = ([], [])
    before = jnp.ones_like(normed)
    current = normed
    slope_before = jnp.zeros_like(normed)
    slope_now = jnp.ones_like(normed)
    for level in range(levels):
        values.append(current)
        slopes.append(slope_now)
        follow = 2.0 * normed * current - before
        slope_follow = 2.0 * current + 2.0 * normed * slope_now - slope_before
        before, current, slope_before, slope_now = (current, follow, slope_now, slope_follow)
    return (jnp.stack(values, 1), jnp.stack(slopes, 1))


def cell_blocks(planes, block_side):
    height, layers, columns = planes.shape
    shaped = planes.reshape(
        height // block_side, block_side, layers, columns // block_side, block_side
    )
    return shaped.transpose(0, 3, 1, 2, 4).reshape(
        height // block_side, columns // block_side, block_side * layers * block_side
    )


def block_cells(blocks, block_side, layers):
    block_rows, block_cols, unused = blocks.shape
    shaped = blocks.reshape(block_rows, block_cols, block_side, layers, block_side)
    return shaped.transpose(0, 2, 3, 1, 4).reshape(
        block_rows * block_side, layers, block_cols * block_side
    )


def field_rows(blocks, block_side, wave_count):
    block_rows, block_cols, unused = blocks.shape
    shaped = blocks.reshape(block_rows, block_cols, block_side, wave_count, 2 * block_side)
    return shaped.transpose(0, 2, 3, 1, 4).reshape(
        block_rows * block_side * wave_count, block_cols * 2 * block_side
    )


def rows_field(row_flat, block_side, wave_count):
    row_count, unused = row_flat.shape
    height = row_count // wave_count
    block_cols = unused // (2 * block_side)
    shaped = row_flat.reshape(
        height // block_side, block_side, wave_count, block_cols, 2 * block_side
    )
    return shaped.transpose(0, 3, 1, 2, 4).reshape(
        height // block_side, block_cols, block_side * wave_count * 2 * block_side
    )


def phase_table(first_col, col_count, total_cols):
    places = first_col + jnp.arange(col_count, dtype=jnp.int32)
    orders = jnp.arange(NK, dtype=jnp.int32) - NK // 2
    phase_turns = places[:, None] * orders[None, :] % total_cols
    angles = phase_turns.astype(jnp.float32) * (2.0 * math.pi / total_cols)
    cosine = jnp.cos(angles)
    sine_part = jnp.sin(angles)
    phase_rows = jnp.stack(
        [jnp.stack([cosine, -sine_part], 1), jnp.stack([sine_part, cosine], 1)], 1
    )
    phase_rows = phase_rows.astype(jnp.bfloat16).reshape(col_count // BS, BS, 2, 2 * NK)
    return phase_rows.transpose(0, 2, 1, 3).reshape(2 * col_count, 2 * NK)


def variation(framed, row_first, col_first, total_rows, total_cols):
    height = framed.shape[0] - 2
    columns = framed.shape[1] - 2
    step_down = framed[1:, :-1] - framed[:-1, :-1]
    step_right = framed[:-1, 1:] - framed[:-1, :-1]
    row_at = row_first - 1 + jnp.arange(height + 1, dtype=jnp.int32)
    col_at = col_first - 1 + jnp.arange(columns + 1, dtype=jnp.int32)
    step_down = jnp.where(((row_at >= 0) & (row_at < total_rows - 1))[:, None], step_down, 0.0)
    step_right = jnp.where(((col_at >= 0) & (col_at < total_cols - 1))[None, :], step_right, 0.0)
    magnitude = jnp.sqrt(step_down * step_down + step_right * step_right + tv_floor)
    flow_down = step_down / magnitude
    flow_right = step_right / magnitude
    return -(flow_down + flow_right)[1:, 1:] + flow_down[:-1, 1:] + flow_right[1:, :-1]


def lane_perm():
    rows = lax.broadcasted_iota(jnp.int32, (OUTS, OUTS), 0)
    cols = lax.broadcasted_iota(jnp.int32, (OUTS, OUTS), 1)
    inner = NW * BS
    hit = (rows // (2 * BS) == cols % inner) & (rows % (2 * BS) == cols // inner)
    return hit.astype(jnp.bfloat16)


def dft_table(total_cols):
    kk = jnp.arange(NK, dtype=jnp.int32) - NK // 2
    low = 8 * BS
    high = total_cols // low
    a = jnp.arange(high, dtype=jnp.int32)
    b = jnp.arange(low, dtype=jnp.int32)
    scale = 2.0 * math.pi / total_cols
    ta = ((a[:, None] * low * kk[None, :]) % total_cols).astype(jnp.float32) * scale
    tb = ((b[:, None] * kk[None, :]) % total_cols).astype(jnp.float32) * scale
    ca, sa = jnp.cos(ta), jnp.sin(ta)
    cb, sb = jnp.cos(tb), jnp.sin(tb)
    cb = cb.reshape(BS, BS, NK).transpose(1, 0, 2)
    sb = sb.reshape(BS, BS, NK).transpose(1, 0, 2)
    cos_v = ca[None, :, None, :] * cb[:, None, :, :] - sa[None, :, None, :] * sb[:, None, :, :]
    sin_v = sa[None, :, None, :] * cb[:, None, :, :] + ca[None, :, None, :] * sb[:, None, :, :]
    cos_v = cos_v.reshape(BS, total_cols // BS, NK)
    sin_v = sin_v.reshape(BS, total_cols // BS, NK)
    return jnp.concatenate([cos_v, sin_v], axis=-1).astype(jnp.bfloat16)


def to_blocks(cells):
    rows, cols = cells.shape
    shaped = cells.reshape(rows // BS, BS, cols // BS, BS).transpose(0, 2, 1, 3)
    return shaped.reshape(rows // BS, cols // BS, BS * BS)


def to_cells(blocks):
    rows, cols, unused = blocks.shape
    shaped = blocks.reshape(rows, cols, BS, BS).transpose(0, 2, 1, 3)
    return shaped.reshape(rows * BS, cols * BS)


def chebyshev_terms(normed, levels):
    values, slopes = ([], [])
    before = jnp.ones_like(normed)
    current = normed
    slope_before = jnp.zeros_like(normed)
    slope_now = jnp.ones_like(normed)
    for level in range(levels):
        values.append(current)
        slopes.append(slope_now)
        follow = 2.0 * normed * current - before
        slope_follow = 2.0 * current + 2.0 * normed * slope_now - slope_before
        before, current, slope_before, slope_now = (current, follow, slope_now, slope_follow)
    return values, slopes


def strip(cells, flags, total_cols, all_by):
    flag_rows = -(-all_by * 9 // total_cols)
    packed = jnp.pad(flags.reshape(-1), (0, flag_rows * total_cols - all_by * 9))
    return jnp.concatenate([cells, packed.reshape(flag_rows, total_cols)])


def unstrip(edge, all_by):
    return edge[:BS], edge[BS:].reshape(-1)[: all_by * 9].reshape(all_by, 9)


def per_device(widths, couplings, surrogate, target_far):
    height, columns = widths.shape
    groups = lax.axis_size("py")
    devices = lax.axis_size("px") * groups
    total_cols = columns * groups
    total_rows = height * lax.axis_size("px")
    rows = height // groups
    own_bx = rows // BS
    all_by = total_cols // BS
    block_cols = columns // BS
    place = lax.axis_index("px") * groups + lax.axis_index("py")
    down = [(i, i + 1) for i in range(devices - 1)]
    up = [(i + 1, i) for i in range(devices - 1)]
    block_rows = height // BS
    flag_vals = block_cols * 9
    flag_rows = -(-flag_vals // columns)
    packed_flags = jnp.pad(
        couplings.astype(jnp.float32).reshape(block_rows, flag_vals),
        ((0, 0), (0, flag_rows * columns - flag_vals)),
    ).reshape(block_rows, flag_rows, columns)
    count = lax.axis_size("px")
    forward = [(i, i + 1) for i in range(count - 1)]
    backward = [(i + 1, i) for i in range(count - 1)]
    low = lax.ppermute(
        jnp.concatenate([widths[height - BS :], packed_flags[block_rows - 1]]), "px", forward
    )
    high = lax.ppermute(jnp.concatenate([widths[:BS], packed_flags[0]]), "px", backward)
    tall_w = jnp.concatenate([low[:BS], widths, high[:BS]])
    tall_f = jnp.concatenate([low[BS:][None], packed_flags, high[BS:][None]])
    win_w = jnp.concatenate(
        [tall_w[:height].reshape(groups, rows, columns), tall_w[2 * BS :].reshape(groups, rows, columns)],
        axis=1,
    )
    win_f = jnp.concatenate(
        [
            tall_f[:block_rows].reshape(groups, own_bx * flag_rows, columns),
            tall_f[2:].reshape(groups, own_bx * flag_rows, columns),
        ],
        axis=1,
    )
    packed = jnp.concatenate([win_w, win_f], axis=1)
    packed, surrogate = lax.optimization_barrier((packed, surrogate))
    depth = packed.shape[1]
    got = lax.all_to_all(packed.reshape(groups * depth, columns), "py", 0, 1, tiled=True)
    rows4 = own_bx + 2
    wide_w = got[: 2 * rows]
    got_flags = got[2 * rows :].reshape(rows4, flag_rows, groups, columns).transpose(0, 2, 1, 3)
    got_flags = got_flags.reshape(rows4, groups, flag_rows * columns)[:, :, :flag_vals]
    wide_flags = got_flags.reshape(rows4, all_by, 9)
    own_flags = wide_flags[1 : own_bx + 1]
    width_blocks = lax.optimization_barrier(to_blocks(wide_w))
    values, unused = chebyshev_terms(width_blocks, NF)
    features = jnp.concatenate(values, axis=-1).astype(jnp.bfloat16)
    sur = surrogate.reshape(9, BS, NF, BS, OUTS).transpose(0, 2, 1, 3, 4).reshape(9, FEAT, OUTS)
    perm = lane_perm()
    sur = jnp.einsum("ofc,cd->ofd", sur, perm, preferred_element_type=jnp.float32).astype(
        jnp.bfloat16
    )
    wide_cols = -(-(all_by + 2) // 16) * 16
    right = wide_cols - all_by - 1
    cells = rows4 * wide_cols
    features = jnp.pad(features, ((0, 0), (1, right), (0, 0)))
    flags16 = jnp.pad(wide_flags.astype(jnp.bfloat16), ((0, 0), (1, right), (0, 0)))
    flat = jnp.pad(features.reshape(cells, FEAT), ((1, 1), (0, 0)))
    flat_flags = jnp.pad(flags16.reshape(cells, 9), ((1, 1), (0, 0)))
    span = own_bx * wide_cols
    pieces = []
    for row_step in range(3):
        for col_step in range(3):
            offset = row_step * 3 + col_step
            first = (2 - row_step) * wide_cols + (2 - col_step)
            pieces.append(
                flat[first : first + span] * flat_flags[first : first + span, offset : offset + 1]
            )
    stacked = jnp.concatenate(pieces, axis=-1)
    near_perm = jnp.dot(
        stacked, sur.reshape(9 * FEAT, OUTS), preferred_element_type=jnp.float32
    ).astype(jnp.bfloat16)
    own_rows = near_perm.reshape(own_bx, wide_cols, OUTS)
    table = jnp.pad(dft_table(total_cols), ((0, 0), (1, right), (0, 0)))
    norm_scale = 1.0 / math.sqrt(total_cols)
    lhs = own_rows.reshape(own_bx, wide_cols, 2, BS, NW * BS)
    parts = jnp.einsum("bYpji,jYq->bpiq", lhs, table, preferred_element_type=jnp.float32)
    real = parts[:, 0, :, :NK] + parts[:, 1, :, NK:]
    imag = parts[:, 1, :, :NK] - parts[:, 0, :, NK:]
    far_field = (jnp.stack([real, imag], axis=2) * norm_scale).reshape(own_bx * BS, NW, 2, NK)
    far_miss = (far_field - target_far.astype(jnp.float32)).astype(jnp.bfloat16)
    framed = jnp.pad(wide_w[BS - 1 : BS + rows + 1], ((0, 0), (1, 1)))
    framed, far_miss = lax.optimization_barrier((framed, far_miss))
    grad_tv = variation(framed, place * rows, 0, total_rows, total_cols)
    miss_above = lax.ppermute(far_miss[BS:], ("px", "py"), down)
    miss_below = lax.ppermute(far_miss[:BS], ("px", "py"), up)
    miss = jnp.concatenate([miss_above, far_miss, miss_below]).reshape(rows4, NW * BS, 2, NK)
    miss_re = miss[:, :, 0]
    miss_im = miss[:, :, 1]
    rhs = jnp.stack(
        [
            jnp.concatenate([miss_re, -miss_im], axis=-1),
            jnp.concatenate([miss_im, miss_re], axis=-1),
        ],
        axis=1,
    )
    adj_flat = jnp.einsum("bpiq,jYq->bYpji", rhs, table, preferred_element_type=jnp.float32)
    wide_adj = (adj_flat * norm_scale).astype(jnp.bfloat16).reshape(rows4, wide_cols, OUTS)
    feat_grad = jnp.zeros((own_bx, all_by, FEAT), jnp.float32)
    for row_step in range(3):
        for col_step in range(3):
            offset = row_step * 3 + col_step
            targets_at = wide_adj[row_step : row_step + own_bx, col_step : col_step + all_by]
            product = jnp.dot(
                targets_at.reshape(own_bx * all_by, OUTS),
                sur[offset].T,
                preferred_element_type=jnp.float32,
            )
            flags = own_flags[:, :, offset]
            feat_grad = feat_grad + flags[:, :, None] * product.reshape(own_bx, all_by, FEAT)
    unused, slopes = chebyshev_terms(width_blocks[1 : own_bx + 1], NF)
    grad_rows = feat_grad[:, :, : BS * BS] * slopes[0]
    for level in range(1, NF):
        grad_rows = grad_rows + feat_grad[:, :, level * BS * BS : (level + 1) * BS * BS] * slopes[level]
    near_grad = to_cells(grad_rows)
    row_grad = near_grad + tv_weight * grad_tv
    width_grad = lax.all_to_all(row_grad, "py", 1, 0, tiled=True)
    return (far_field, width_grad)


def solution(mesh):
    return jax.shard_map(
        per_device,
        mesh=mesh,
        in_specs=(P("px", "py"), P("px", "py", None), P(), P(("px", "py"), None, None, None)),
        out_specs=(P(("px", "py"), None, None, None), P("px", "py")),
        check_vma=False,
    )
```
